32 devices in a mesh: px: 4 (over y, x), py: 8 (over z, core).
Axes of the slice: x: 2, y: 2, z: 4, core: 2. Of those that a mesh axis runs over, the one named last changes fastest.
Arguments:
- residual: float32 [10, 2048, 2048], P(None, 'py', 'px'), may hold values from -6 to 6
- lambda_x: float32 [2048], P('px'), may hold values from 0.1 to 4
- lambda_y: float32 [2048], P('py'), may hold values from 0.1 to 4
- coupling: float32 [9], replicated, may hold values from 0.2 to 2
- layer_shift: float32 [10], replicated, may hold values from 0.05 to 1
- left_x: bfloat16 [2048, 2048], P(None, 'px'), may hold values from -0.125 to 0.125
- left_y: bfloat16 [2048, 2048], P('py'), may hold values from -0.125 to 0.125
- right_y: bfloat16 [2048, 2048], P('py'), may hold values from -0.125 to 0.125
- right_x: bfloat16 [2048, 2048], P(None, 'px'), may hold values from -0.125 to 0.125
- regime_code: int32 [10, 2048, 2048], P(None, 'py', 'px'), may hold values from 0 to 3
- upwind_flag: int32 [2, 10, 2048, 2048], P(None, None, 'py', 'px'), may hold values from 0 to 1
- mobility_table: float32 [4], replicated, may hold values from 0.3 to 3
Outputs:
- correction: float32 [10, 2048, 2048], P(None, 'py', 'px')
- balance: float32 [10, 2048, 2048], P(None, 'py', 'px')
The draws below stay inside these ranges and needn't reach their ends.
Inputs may be any that keep to these rules, and one draw needn't show every extreme that they name: `regime_code`: a regime number of each cell.
All inputs are finite; a program needn't handle non-finite values.
Results may differ from the reference program's by a relative error of at most 0.0057.
Values may be sent and summed in bfloat16 or wider, within the bound.
No kernel may reach another device: no remote copies, remote signals or barrier semaphores. Data moves between devices by JAX's collectives and lax.ppermute only.
A program may use at most 192 MiB of HBM per device.

```python
import math
import jax
import jax.numpy as jnp

NX = 2048
NY = 2048
LAYERS = 10
REGIMES = 4


def plant(drawn, key, smallest, largest):
    place = [jax.random.randint(jax.random.fold_in(key, axis), (), 0, length) for axis, length in enumerate(drawn.shape)]
    widest = drawn.shape.index(max(drawn.shape))
    next_to = place[:widest] + [(place[widest] + 1) % drawn.shape[widest]] + place[widest + 1:]
    return drawn.at[tuple(place)].set(smallest).at[tuple(next_to)].set(largest)


def levels(rng, extent, split, smallest, top_value):
    level, own = 1.0, jax.random.fold_in(rng, 6)
    for axis_at, shards_of in split:
        steps = jnp.exp(jax.random.uniform(jax.random.fold_in(own, axis_at), (shards_of,), jnp.float32, smallest / len(split), top_value / len(split)))
        level = level * jnp.repeat(steps, extent[axis_at] // shards_of).reshape([-1 if axis == axis_at else 1 for axis in range(len(extent))])
    return level


def bell_draw(own_key, extent, scale, reach, shards=(), kind=jnp.bfloat16):
    result = scale * jax.random.normal(own_key, extent, jnp.float32)
    if shards:
        result = result * levels(own_key, extent, shards, -0.22, 0.18)
    return jnp.clip(result, -reach, reach).astype(kind)


def setup_inputs(seed: int = 0) -> dict:
    seeds = jax.random.split(jax.random.key(seed), 13)
    return {
        "residual": bell_draw(seeds[0], (LAYERS, NY, NX), 1.0, 6.0, ((1, 8), (2, 4)), jnp.float32),
        "lambda_x": jnp.clip(jnp.exp(math.log(4.0) - 3.6888794 * jax.random.uniform(seeds[1], (NX,), jnp.float32) ** levels(seeds[1], (NX,), ((0, 4),), -0.2, 0.2)), 0.1, 4.0),
        "lambda_y": jnp.clip(jnp.exp(math.log(4.0) - 3.6888794 * jax.random.uniform(seeds[2], (NY,), jnp.float32) ** levels(seeds[2], (NY,), ((0, 8),), -0.2, 0.2)), 0.1, 4.0),
        "coupling": jnp.clip(jnp.exp(jax.random.uniform(seeds[3], (LAYERS - 1,), jnp.float32, math.log(0.2), math.log(2.0))), 0.2, 2.0),
        "layer_shift": jnp.clip(jnp.exp(jax.random.uniform(seeds[4], (LAYERS,), jnp.float32, math.log(0.05), math.log(1.0))), 0.05, 1.0),
        "left_x": bell_draw(seeds[5], (NX, NX), NX ** -0.5, 0.125, ((1, 4),)),
        "left_y": bell_draw(seeds[6], (NY, NY), NY ** -0.5, 0.125, ((0, 8),)),
        "right_y": bell_draw(seeds[7], (NY, NY), NY ** -0.5, 0.125, ((0, 8),)),
        "right_x": bell_draw(seeds[8], (NX, NX), NX ** -0.5, 0.125, ((1, 4),)),
        "regime_code": plant(jax.random.randint(seeds[9], (LAYERS, NY, NX), 0, REGIMES), jax.random.fold_in(seeds[9], 1), 0, REGIMES - 1).astype(jnp.int32),
        "upwind_flag": plant(jax.random.randint(seeds[10], (2, LAYERS, NY, NX), 0, 2), jax.random.fold_in(seeds[10], 1), 0, 1).astype(jnp.int32),
        "mobility_table": jnp.clip(jnp.exp(jax.random.uniform(seeds[11], (REGIMES,), jnp.float32, math.log(0.3), math.log(3.0))), 0.3, 3.0),
    }


def thomas_solve(rhs, lambda_x, lambda_y, coupling, layer_shift):
    layers = rhs.shape[0]
    mode_sum = lambda_y[:, None] + lambda_x[None, :]
    ratios = []
    partial_values = []
    for layer_index in range(layers):
        diagonal = mode_sum + layer_shift[layer_index]
        if layer_index > 0:
            diagonal = diagonal + coupling[layer_index - 1]
        if layer_index < layers - 1:
            diagonal = diagonal + coupling[layer_index]
        if layer_index == 0:
            pivots = diagonal
            solved = rhs[0] / pivots
        else:
            pivots = diagonal + coupling[layer_index - 1] * ratios[-1]
            solved = (rhs[layer_index] + coupling[layer_index - 1] * partial_values[-1]) / pivots
        partial_values.append(solved)
        if layer_index < layers - 1:
            ratios.append(-coupling[layer_index] / pivots)
    results = [partial_values[layers - 1]]
    for layer_index in range(layers - 2, -1, -1):
        results.append(partial_values[layer_index] - ratios[layer_index] * results[-1])
    return jnp.stack(results[::-1])


def lookup(regime_code, mobility_table):
    mobility = jnp.zeros(regime_code.shape, jnp.float32)
    for regime in range(mobility_table.shape[0]):
        mobility = jnp.where(regime_code == regime, mobility_table[regime], mobility)
    return mobility


def reference(residual, lambda_x, lambda_y, coupling, layer_shift, left_x, left_y, right_y, right_x, regime_code, upwind_flag, mobility_table):
    rounded = residual.astype(jnp.bfloat16)
    spectral_x = jnp.einsum('zyx,xi->zyi', rounded.astype(jnp.float32), left_x.astype(jnp.float32)).astype(jnp.bfloat16)
    spectral = jnp.einsum('jy,zyi->zji', left_y.astype(jnp.float32), spectral_x.astype(jnp.float32))
    solved = thomas_solve(spectral, lambda_x, lambda_y, coupling, layer_shift).astype(jnp.bfloat16)
    back_y = jnp.einsum('yj,zji->zyi', right_y.astype(jnp.float32), solved.astype(jnp.float32)).astype(jnp.bfloat16)
    correction = jnp.einsum('zyi,ix->zyx', back_y.astype(jnp.float32), right_x.astype(jnp.float32))
    mobility = lookup(regime_code, mobility_table)
    upwind_x = jnp.where(upwind_flag[0][:, :, :-1] == 1, mobility[:, :, :-1], mobility[:, :, 1:])
    flux_x = upwind_x * (correction[:, :, :-1] - correction[:, :, 1:])
    net_x = jnp.pad(flux_x, ((0, 0), (0, 0), (0, 1))) - jnp.pad(flux_x, ((0, 0), (0, 0), (1, 0)))
    upwind_y = jnp.where(upwind_flag[1][:, :-1, :] == 1, mobility[:, :-1, :], mobility[:, 1:, :])
    flux_y = upwind_y * (correction[:, :-1, :] - correction[:, 1:, :])
    net_y = jnp.pad(flux_y, ((0, 0), (0, 1), (0, 0))) - jnp.pad(flux_y, ((0, 0), (1, 0), (0, 0)))
    balance = net_x + net_y
    return (correction, balance)
```

```python
import jax
import jax.numpy as jnp
from jax import lax
from jax.sharding import PartitionSpec as P


def with_halo(block, sides, width):
    for axis, dim in sides:
        count = lax.axis_size(axis)
        forward = [(i, i + 1) for i in range(count - 1)]
        backward = [(target, source) for source, target in forward]
        low = lax.ppermute(
            lax.slice_in_dim(block, block.shape[dim] - width, None, axis=dim), axis, forward
        )
        high = lax.ppermute(lax.slice_in_dim(block, 0, width, axis=dim), axis, backward)
        block = jnp.concatenate([low, block, high], axis=dim)
    return block


def thomas_solve(rhs, lambda_x, lambda_y, coupling, layer_shift):
    layers = rhs.shape[0]
    mode_sum = lambda_y[:, None] + lambda_x[None, :]
    ratios = []
    partial_values = []
    for layer_index in range(layers):
        diagonal = mode_sum + layer_shift[layer_index]
        if layer_index > 0:
            diagonal = diagonal + coupling[layer_index - 1]
        if layer_index < layers - 1:
            diagonal = diagonal + coupling[layer_index]
        if layer_index == 0:
            pivots = diagonal
            solved = rhs[0] / pivots
        else:
            pivots = diagonal + coupling[layer_index - 1] * ratios[-1]
            solved = (rhs[layer_index] + coupling[layer_index - 1] * partial_values[-1]) / pivots
        partial_values.append(solved)
        if layer_index < layers - 1:
            ratios.append(-coupling[layer_index] / pivots)
    results = [partial_values[layers - 1]]
    for layer_index in range(layers - 2, -1, -1):
        results.append(partial_values[layer_index] - ratios[layer_index] * results[-1])
    return jnp.stack(results[::-1])


def shards(
    residual,
    lambda_x,
    lambda_y,
    coupling,
    layer_shift,
    left_x,
    left_y,
    right_y,
    right_x,
    regime_code,
    upwind_flag,
    mobility_table,
):
    count_y = lax.axis_size("py")
    rounded = residual.astype(jnp.bfloat16)
    spectral_x = jnp.einsum(
        "zyx,xi->zyi",
        lax.all_gather(rounded, "px", axis=2, tiled=True),
        left_x,
        preferred_element_type=jnp.float32,
    ).astype(jnp.bfloat16)
    pencil = lax.all_to_all(spectral_x, "py", 2, 1, tiled=True)
    modes = pencil.shape[2]
    spectral = jnp.einsum(
        "jy,zyi->zji",
        lax.all_gather(left_y, "py", axis=0, tiled=True),
        pencil,
        preferred_element_type=jnp.float32,
    )
    own_x = lax.dynamic_slice_in_dim(lambda_x, lax.axis_index("py") * modes, modes)
    all_y = lax.all_gather(lambda_y, "py", axis=0, tiled=True)
    solved = thomas_solve(spectral, own_x, all_y, coupling, layer_shift).astype(jnp.bfloat16)
    back_pencil = jnp.einsum(
        "yj,zji->zyi",
        lax.all_gather(right_y, "py", axis=0, tiled=True),
        solved,
        preferred_element_type=jnp.float32,
    ).astype(jnp.bfloat16)
    back_y = lax.all_to_all(back_pencil, "py", 1, 2, tiled=True)
    del count_y

    mobility = jnp.zeros(regime_code.shape, jnp.float32)
    for regime in range(mobility_table.shape[0]):
        mobility = jnp.where(regime_code == regime, mobility_table[regime], mobility)
    correction = jnp.einsum(
        "zyi,ix->zyx",
        lax.all_gather(back_y, "px", axis=2, tiled=True),
        right_x,
        preferred_element_type=jnp.float32,
    )
    width_x = correction.shape[2]
    width_y = correction.shape[1]
    stacked = jnp.stack(
        [
            correction,
            mobility,
            upwind_flag[0].astype(jnp.float32),
            upwind_flag[1].astype(jnp.float32),
        ]
    )
    extended = with_halo(stacked, (("px", 3), ("py", 2)), 1)
    press_x = extended[0][:, 1:-1, :]
    mobil_x = extended[1][:, 1:-1, :]
    flags_x = extended[2][:, 1:-1, :]
    upwind_x = jnp.where(flags_x[:, :, :-1] > 0.5, mobil_x[:, :, :-1], mobil_x[:, :, 1:])
    flux_x = upwind_x * (press_x[:, :, :-1] - press_x[:, :, 1:])
    faces_x = lax.axis_index("px") * width_x + jnp.arange(width_x + 1, dtype=jnp.int32)
    valid_x = (faces_x >= 1) & (faces_x <= width_x * lax.axis_size("px") - 1)
    flux_x = jnp.where(valid_x[None, None, :], flux_x, 0.0)
    net_x = flux_x[:, :, 1:] - flux_x[:, :, :-1]
    press_y = extended[0][:, :, 1:-1]
    mobil_y = extended[1][:, :, 1:-1]
    flags_y = extended[3][:, :, 1:-1]
    upwind_y = jnp.where(flags_y[:, :-1, :] > 0.5, mobil_y[:, :-1, :], mobil_y[:, 1:, :])
    flux_y = upwind_y * (press_y[:, :-1, :] - press_y[:, 1:, :])
    faces_y = lax.axis_index("py") * width_y + jnp.arange(width_y + 1, dtype=jnp.int32)
    valid_y = (faces_y >= 1) & (faces_y <= width_y * lax.axis_size("py") - 1)
    flux_y = jnp.where(valid_y[None, :, None], flux_y, 0.0)
    net_y = flux_y[:, 1:, :] - flux_y[:, :-1, :]
    balance = net_x + net_y
    return (correction, balance)


def solution(mesh):
    return jax.shard_map(
        shards,
        mesh=mesh,
        in_specs=(
            P(None, "py", "px"),
            P("px"),
            P("py"),
            P(),
            P(),
            P(None, "px"),
            P("py", None),
            P("py", None),
            P(None, "px"),
            P(None, "py", "px"),
            P(None, None, "py", "px"),
            P(),
        ),
        out_specs=(P(None, "py", "px"), P(None, "py", "px")),
        check_vma=False,
    )
```

```python
import jax
import jax.numpy as jnp
from jax import lax
from jax.experimental import pallas as pl
from jax.experimental.pallas import tpu as pltpu
from jax.sharding import PartitionSpec as P


def exchange(block, axis):
    count = lax.axis_size(axis)
    parts = [block]
    for k in range(1, count):
        parts.append(lax.ppermute(block, axis, [(s, s ^ k) for s in range(count)]))
    return parts


def in_exchange_order(matrix, axis):
    count = lax.axis_size(axis)
    own = lax.axis_index(axis)
    blocks = matrix.reshape(count, matrix.shape[0] // count, matrix.shape[1])
    return jnp.concatenate(
        [lax.dynamic_index_in_dim(blocks, own ^ k, 0, keepdims=False) for k in range(count)]
    )


def thomas_kernel(coupling_ref, shift_ref, ly_ref, lx_ref, rhs_ref, out_ref):
    layers = rhs_ref.shape[0]
    mode_sum = ly_ref[...] + lx_ref[...]
    ratios = []
    partial_values = []
    for layer_index in range(layers):
        diagonal = mode_sum + shift_ref[layer_index]
        if layer_index > 0:
            diagonal = diagonal + coupling_ref[layer_index - 1]
        if layer_index < layers - 1:
            diagonal = diagonal + coupling_ref[layer_index]
        if layer_index == 0:
            pivots = diagonal
            solved = rhs_ref[0] / pivots
        else:
            pivots = diagonal + coupling_ref[layer_index - 1] * ratios[-1]
            solved = (rhs_ref[layer_index] + coupling_ref[layer_index - 1] * partial_values[-1]) / pivots
        partial_values.append(solved)
        if layer_index < layers - 1:
            ratios.append(-coupling_ref[layer_index] / pivots)
    result = partial_values[layers - 1]
    out_ref[layers - 1] = result.astype(out_ref.dtype)
    for layer_index in range(layers - 2, -1, -1):
        result = partial_values[layer_index] - ratios[layer_index] * result
        out_ref[layer_index] = result.astype(out_ref.dtype)


def thomas_solve(rhs, lambda_x, lambda_y, coupling, layer_shift):
    layers, rows, modes = rhs.shape
    tile = min(rows, 256)
    smem = pl.BlockSpec(memory_space=pltpu.SMEM)
    return pl.pallas_call(
        thomas_kernel,
        grid=(rows // tile,),
        in_specs=[
            smem,
            smem,
            pl.BlockSpec((tile, 1), lambda j: (j, 0)),
            pl.BlockSpec((1, modes), lambda j: (0, 0)),
            pl.BlockSpec((layers, tile, modes), lambda j: (0, j, 0)),
        ],
        out_specs=pl.BlockSpec((layers, tile, modes), lambda j: (0, j, 0)),
        out_shape=jax.ShapeDtypeStruct(rhs.shape, jnp.bfloat16),
    )(coupling, layer_shift, lambda_y.reshape(rows, 1), lambda_x.reshape(1, modes), rhs)


def shards(
    residual,
    lambda_x,
    lambda_y,
    coupling,
    layer_shift,
    left_x,
    left_y,
    right_y,
    right_x,
    regime_code,
    upwind_flag,
    mobility_table,
):
    count_x = lax.axis_size("px")
    count_y = lax.axis_size("py")
    at_x = lax.axis_index("px")
    at_y = lax.axis_index("py")
    layers, height, width = residual.shape
    modes = left_x.shape[1] // count_y

    rounded = residual.astype(jnp.bfloat16)
    spectral_x = jnp.einsum(
        "zyx,xci->czyi",
        jnp.concatenate(exchange(rounded, "px"), axis=2),
        in_exchange_order(left_x, "px").reshape(-1, count_y, modes),
        preferred_element_type=jnp.float32,
    ).astype(jnp.bfloat16)
    pencil = lax.all_to_all(spectral_x, "py", 0, 0, tiled=True)
    spectral = jnp.einsum(
        "jsy,szyi->zji",
        lax.all_gather(left_y, "py", axis=0, tiled=True).reshape(-1, count_y, height),
        pencil,
        preferred_element_type=jnp.float32,
    )
    own_x = lax.dynamic_slice_in_dim(lambda_x, at_y * modes, modes)
    spread_y = jnp.zeros((count_y, lambda_y.shape[0]), lambda_y.dtype)
    spread_y = lax.dynamic_update_index_in_dim(spread_y, lambda_y, at_y, 0)
    all_y = lax.psum(spread_y, "py").reshape(-1)
    solved = thomas_solve(spectral, own_x, all_y, coupling, layer_shift)
    back_pencil = jnp.einsum(
        "syj,zji->szyi",
        lax.all_gather(right_y, "py", axis=0, tiled=True).reshape(count_y, height, -1),
        solved,
        preferred_element_type=jnp.float32,
    ).astype(jnp.bfloat16)
    back_y = lax.all_to_all(back_pencil, "py", 0, 0, tiled=True)
    back_y = jnp.moveaxis(back_y, 0, 2).reshape(layers, height, -1)
    correction = jnp.einsum(
        "zyi,ix->zyx",
        jnp.concatenate(exchange(back_y, "px"), axis=2),
        in_exchange_order(right_x, "px"),
        preferred_element_type=jnp.float32,
    )

    mobility = jnp.zeros(regime_code.shape, jnp.float32)
    for regime in range(mobility_table.shape[0]):
        mobility = jnp.where(regime_code == regime, mobility_table[regime], mobility)
    flag_x = upwind_flag[0]
    flag_y = upwind_flag[1]

    def net(axis, dim, flag, at, count):
        forward = [(i, i + 1) for i in range(count - 1)]
        backward = [(i + 1, i) for i in range(count - 1)]
        first = lambda a: lax.slice_in_dim(a, 0, 1, axis=dim)
        last = lambda a: lax.slice_in_dim(a, a.shape[dim] - 1, None, axis=dim)
        rest = lambda a: lax.slice_in_dim(a, 1, None, axis=dim)
        head = lambda a: lax.slice_in_dim(a, 0, a.shape[dim] - 1, axis=dim)
        high = lax.ppermute(jnp.stack([first(correction), first(mobility)]), axis, backward)
        low = lax.ppermute(
            jnp.stack([last(correction), last(mobility), last(flag).astype(jnp.float32)]), axis, forward
        )
        press_next = jnp.concatenate([rest(correction), high[0]], axis=dim)
        mobil_next = jnp.concatenate([rest(mobility), high[1]], axis=dim)
        flux_high = jnp.where(flag == 1, mobility, mobil_next) * (correction - press_next)
        place = lax.broadcasted_iota(jnp.int32, correction.shape, dim)
        edge = (at == count - 1) & (place == correction.shape[dim] - 1)
        flux_high = jnp.where(edge, 0.0, flux_high)
        flux_edge = jnp.where(low[2] > 0.5, low[1], first(mobility)) * (low[0] - first(correction))
        flux_edge = jnp.where(at == 0, 0.0, flux_edge)
        flux_low = jnp.concatenate([flux_edge, head(flux_high)], axis=dim)
        return flux_high - flux_low

    balance = net("px", 2, flag_x, at_x, count_x) + net("py", 1, flag_y, at_y, count_y)
    return (correction, balance)


def solution(mesh):
    return jax.shard_map(
        shards,
        mesh=mesh,
        in_specs=(
            P(None, "py", "px"),
            P("px"),
            P("py"),
            P(),
            P(),
            P(None, "px"),
            P("py", None),
            P("py", None),
            P(None, "px"),
            P(None, "py", "px"),
            P(None, None, "py", "px"),
            P(),
        ),
        out_specs=(P(None, "py", "px"), P(None, "py", "px")),
        check_vma=False,
    )
```

```python
import jax
import jax.numpy as jnp
from jax import lax
from jax.experimental import pallas as pl
from jax.experimental.pallas import tpu as pltpu
from jax.sharding import PartitionSpec as P


def exchange(block, axis):
    count = lax.axis_size(axis)
    parts = [block]
    for k in range(1, count):
        parts.append(lax.ppermute(block, axis, [(s, s ^ k) for s in range(count)]))
    return parts


def in_exchange_order(matrix, axis):
    count = lax.axis_size(axis)
    own = lax.axis_index(axis)
    blocks = matrix.reshape(count, matrix.shape[0] // count, matrix.shape[1])
    return jnp.concatenate(
        [lax.dynamic_index_in_dim(blocks, own ^ k, 0, keepdims=False) for k in range(count)]
    )


def thomas_kernel(coupling_ref, shift_ref, ly_ref, lx_ref, rhs_ref, out_ref):
    layers = rhs_ref.shape[0]
    mode_sum = ly_ref[...] + lx_ref[...]
    ratios = []
    partial_values = []
    for layer_index in range(layers):
        diagonal = mode_sum + shift_ref[layer_index]
        if layer_index > 0:
            diagonal = diagonal + coupling_ref[layer_index - 1]
        if layer_index < layers - 1:
            diagonal = diagonal + coupling_ref[layer_index]
        if layer_index == 0:
            pivots = diagonal
            solved = rhs_ref[0] / pivots
        else:
            pivots = diagonal + coupling_ref[layer_index - 1] * ratios[-1]
            solved = (rhs_ref[layer_index] + coupling_ref[layer_index - 1] * partial_values[-1]) / pivots
        partial_values.append(solved)
        if layer_index < layers - 1:
            ratios.append(-coupling_ref[layer_index] / pivots)
    result = partial_values[layers - 1]
    out_ref[layers - 1] = result.astype(out_ref.dtype)
    for layer_index in range(layers - 2, -1, -1):
        result = partial_values[layer_index] - ratios[layer_index] * result
        out_ref[layer_index] = result.astype(out_ref.dtype)


def thomas_solve(rhs, lambda_x, lambda_y, coupling, layer_shift):
    layers, rows, modes = rhs.shape
    tile = min(rows, 256)
    smem = pl.BlockSpec(memory_space=pltpu.SMEM)
    return pl.pallas_call(
        thomas_kernel,
        grid=(rows // tile,),
        in_specs=[
            smem,
            smem,
            pl.BlockSpec((tile, 1), lambda j: (j, 0)),
            pl.BlockSpec((1, modes), lambda j: (0, 0)),
            pl.BlockSpec((layers, tile, modes), lambda j: (0, j, 0)),
        ],
        out_specs=pl.BlockSpec((layers, tile, modes), lambda j: (0, j, 0)),
        out_shape=jax.ShapeDtypeStruct(rhs.shape, jnp.bfloat16),
    )(coupling, layer_shift, lambda_y.reshape(rows, 1), lambda_x.reshape(1, modes), rhs)


def shards(
    residual,
    lambda_x,
    lambda_y,
    coupling,
    layer_shift,
    left_x,
    left_y,
    right_y,
    right_x,
    regime_code,
    upwind_flag,
    mobility_table,
):
    count_x = lax.axis_size("px")
    count_y = lax.axis_size("py")
    at_x = lax.axis_index("px")
    at_y = lax.axis_index("py")
    layers, height, width = residual.shape
    modes = left_x.shape[1] // count_y

    rounded = residual.astype(jnp.bfloat16)
    spectral_x = jnp.einsum(
        "zyx,xci->czyi",
        jnp.concatenate(exchange(rounded, "px"), axis=2),
        in_exchange_order(left_x, "px").reshape(-1, count_y, modes),
        preferred_element_type=jnp.float32,
    ).astype(jnp.bfloat16)
    pencil = lax.all_to_all(spectral_x, "py", 0, 0, tiled=True)
    high = lambda_y.astype(jnp.bfloat16)
    rest = lambda_y - high.astype(jnp.float32)
    middle = rest.astype(jnp.bfloat16)
    low = (rest - middle.astype(jnp.float32)).astype(jnp.bfloat16)
    pieces = jnp.zeros((lambda_y.shape[0], 128), jnp.bfloat16)
    pieces = pieces.at[:, 0].set(high).at[:, 1].set(middle).at[:, 2].set(low)
    carried = lax.all_gather(jnp.concatenate([left_y, pieces], axis=1), "py", axis=0, tiled=True)
    columns = left_y.shape[1]
    spectral = jnp.einsum(
        "jsy,szyi->zji",
        carried[:, :columns].reshape(-1, count_y, height),
        pencil,
        preferred_element_type=jnp.float32,
    )
    own_x = lax.dynamic_slice_in_dim(lambda_x, at_y * modes, modes)
    got = carried[:, columns:columns + 3].astype(jnp.float32)
    all_y = got[:, 0] + (got[:, 1] + got[:, 2])
    solved = thomas_solve(spectral, own_x, all_y, coupling, layer_shift)
    back_pencil = jnp.einsum(
        "syj,zji->szyi",
        lax.all_gather(right_y, "py", axis=0, tiled=True).reshape(count_y, height, -1),
        solved,
        preferred_element_type=jnp.float32,
    ).astype(jnp.bfloat16)
    back_y = lax.all_to_all(back_pencil, "py", 0, 0, tiled=True)
    back_y = jnp.moveaxis(back_y, 0, 2).reshape(layers, height, -1)
    correction = jnp.einsum(
        "zyi,ix->zyx",
        lax.all_gather(back_y, "px", axis=2, tiled=True),
        right_x,
        preferred_element_type=jnp.float32,
    )

    mobility = jnp.zeros(regime_code.shape, jnp.float32)
    for regime in range(mobility_table.shape[0]):
        mobility = jnp.where(regime_code == regime, mobility_table[regime], mobility)
    flag_x = upwind_flag[0]
    flag_y = upwind_flag[1]

    def net(axis, dim, flag, at, count):
        forward = [(i, i + 1) for i in range(count - 1)]
        backward = [(i + 1, i) for i in range(count - 1)]
        first = lambda a: lax.slice_in_dim(a, 0, 1, axis=dim)
        last = lambda a: lax.slice_in_dim(a, a.shape[dim] - 1, None, axis=dim)
        rest = lambda a: lax.slice_in_dim(a, 1, None, axis=dim)
        head = lambda a: lax.slice_in_dim(a, 0, a.shape[dim] - 1, axis=dim)
        high = lax.ppermute(jnp.stack([first(correction), first(mobility)]), axis, backward)
        low = lax.ppermute(
            jnp.stack([last(correction), last(mobility), last(flag).astype(jnp.float32)]), axis, forward
        )
        press_next = jnp.concatenate([rest(correction), high[0]], axis=dim)
        mobil_next = jnp.concatenate([rest(mobility), high[1]], axis=dim)
        flux_high = jnp.where(flag == 1, mobility, mobil_next) * (correction - press_next)
        place = lax.broadcasted_iota(jnp.int32, correction.shape, dim)
        edge = (at == count - 1) & (place == correction.shape[dim] - 1)
        flux_high = jnp.where(edge, 0.0, flux_high)
        flux_edge = jnp.where(low[2] > 0.5, low[1], first(mobility)) * (low[0] - first(correction))
        flux_edge = jnp.where(at == 0, 0.0, flux_edge)
        flux_low = jnp.concatenate([flux_edge, head(flux_high)], axis=dim)
        return flux_high - flux_low

    balance = net("px", 2, flag_x, at_x, count_x) + net("py", 1, flag_y, at_y, count_y)
    return (correction, balance)


def solution(mesh):
    return jax.shard_map(
        shards,
        mesh=mesh,
        in_specs=(
            P(None, "py", "px"),
            P("px"),
            P("py"),
            P(),
            P(),
            P(None, "px"),
            P("py", None),
            P("py", None),
            P(None, "px"),
            P(None, "py", "px"),
            P(None, None, "py", "px"),
            P(),
        ),
        out_specs=(P(None, "py", "px"), P(None, "py", "px")),
        check_vma=False,
    )
```

```python
import jax
import jax.numpy as jnp
from jax import lax
from jax.experimental import pallas as pl
from jax.experimental.pallas import tpu as pltpu
from jax.sharding import PartitionSpec as P


def exchange(block, axis):
    count = lax.axis_size(axis)
    parts = [block]
    for k in range(1, count):
        parts.append(lax.ppermute(block, axis, [(s, s ^ k) for s in range(count)]))
    return parts


def arrange(received, axis):
    own = lax.axis_index(axis)
    stacked = jnp.stack(received)
    return jnp.stack(
        [lax.dynamic_index_in_dim(stacked, own ^ s, 0, keepdims=False) for s in range(len(received))]
    )


def chip_gather(block, axis):
    count = lax.axis_size(axis)
    same_core = [block]
    for k in range(2, count, 2):
        same_core.append(lax.ppermute(block, axis, [(s, s ^ k) for s in range(count)]))
    mine = jnp.stack(same_core)
    other = lax.ppermute(mine, axis, [(s, s ^ 1) for s in range(count)])
    received = [None] * count
    for k in range(0, count, 2):
        received[k] = mine[k // 2]
        received[k + 1] = other[k // 2]
    return arrange(received, axis)


def swap_chunks(chunks, axis):
    count = lax.axis_size(axis)
    own = lax.axis_index(axis)
    received = [lax.dynamic_index_in_dim(chunks, own, 0, keepdims=False)]
    for k in range(1, count):
        piece = lax.dynamic_index_in_dim(chunks, own ^ k, 0, keepdims=False)
        received.append(lax.ppermute(piece, axis, [(s, s ^ k) for s in range(count)]))
    return arrange(received, axis)


def in_exchange_order(matrix, axis):
    count = lax.axis_size(axis)
    own = lax.axis_index(axis)
    blocks = matrix.reshape(count, matrix.shape[0] // count, matrix.shape[1])
    return jnp.concatenate(
        [lax.dynamic_index_in_dim(blocks, own ^ k, 0, keepdims=False) for k in range(count)]
    )


def thomas_kernel(coupling_ref, shift_ref, ly_ref, lx_ref, rhs_ref, out_ref):
    layers = rhs_ref.shape[0]
    mode_sum = ly_ref[...] + lx_ref[...]
    ratios = []
    partial_values = []
    for layer_index in range(layers):
        diagonal = mode_sum + shift_ref[layer_index]
        if layer_index > 0:
            diagonal = diagonal + coupling_ref[layer_index - 1]
        if layer_index < layers - 1:
            diagonal = diagonal + coupling_ref[layer_index]
        if layer_index == 0:
            pivots = diagonal
            solved = rhs_ref[0] / pivots
        else:
            pivots = diagonal + coupling_ref[layer_index - 1] * ratios[-1]
            solved = (rhs_ref[layer_index] + coupling_ref[layer_index - 1] * partial_values[-1]) / pivots
        partial_values.append(solved)
        if layer_index < layers - 1:
            ratios.append(-coupling_ref[layer_index] / pivots)
    result = partial_values[layers - 1]
    out_ref[layers - 1] = result.astype(out_ref.dtype)
    for layer_index in range(layers - 2, -1, -1):
        result = partial_values[layer_index] - ratios[layer_index] * result
        out_ref[layer_index] = result.astype(out_ref.dtype)


def thomas_solve(rhs, lambda_x, lambda_y, coupling, layer_shift):
    layers, rows, modes = rhs.shape
    tile = min(rows, 256)
    smem = pl.BlockSpec(memory_space=pltpu.SMEM)
    return pl.pallas_call(
        thomas_kernel,
        grid=(rows // tile,),
        in_specs=[
            smem,
            smem,
            pl.BlockSpec((tile, 1), lambda j: (j, 0)),
            pl.BlockSpec((1, modes), lambda j: (0, 0)),
            pl.BlockSpec((layers, tile, modes), lambda j: (0, j, 0)),
        ],
        out_specs=pl.BlockSpec((layers, tile, modes), lambda j: (0, j, 0)),
        out_shape=jax.ShapeDtypeStruct(rhs.shape, jnp.bfloat16),
    )(coupling, layer_shift, lambda_y.reshape(rows, 1), lambda_x.reshape(1, modes), rhs)


def shards(
    residual,
    lambda_x,
    lambda_y,
    coupling,
    layer_shift,
    left_x,
    left_y,
    right_y,
    right_x,
    regime_code,
    upwind_flag,
    mobility_table,
):
    count_x = lax.axis_size("px")
    count_y = lax.axis_size("py")
    at_x = lax.axis_index("px")
    at_y = lax.axis_index("py")
    layers, height, width = residual.shape
    modes = left_x.shape[1] // count_y

    rounded = residual.astype(jnp.bfloat16)
    spectral_x = jnp.einsum(
        "zyx,xci->czyi",
        jnp.concatenate(exchange(rounded, "px"), axis=2),
        in_exchange_order(left_x, "px").reshape(-1, count_y, modes),
        preferred_element_type=jnp.float32,
    ).astype(jnp.bfloat16)
    pencil = swap_chunks(spectral_x, "py")
    spectral = jnp.einsum(
        "sjty,tzyi->zsji",
        chip_gather(left_y, "py").reshape(count_y, -1, count_y, height),
        pencil,
        preferred_element_type=jnp.float32,
    ).reshape(layers, -1, modes)
    own_x = lax.dynamic_slice_in_dim(lambda_x, at_y * modes, modes)
    all_y = chip_gather(lambda_y, "py").reshape(-1)
    solved = thomas_solve(spectral, own_x, all_y, coupling, layer_shift)
    back_pencil = jnp.einsum(
        "syj,zji->szyi",
        chip_gather(right_y, "py"),
        solved,
        preferred_element_type=jnp.float32,
    ).astype(jnp.bfloat16)
    back_y = swap_chunks(back_pencil, "py")
    back_y = jnp.moveaxis(back_y, 0, 2).reshape(layers, height, -1)
    correction = jnp.einsum(
        "zyi,ix->zyx",
        lax.all_gather(back_y, "px", axis=2, tiled=True),
        right_x,
        preferred_element_type=jnp.float32,
    )

    mobility = jnp.zeros(regime_code.shape, jnp.float32)
    for regime in range(mobility_table.shape[0]):
        mobility = jnp.where(regime_code == regime, mobility_table[regime], mobility)
    flag_x = upwind_flag[0]
    flag_y = upwind_flag[1]

    def net(axis, dim, flag, at, count):
        forward = [(i, i + 1) for i in range(count - 1)]
        backward = [(i + 1, i) for i in range(count - 1)]
        first = lambda a: lax.slice_in_dim(a, 0, 1, axis=dim)
        last = lambda a: lax.slice_in_dim(a, a.shape[dim] - 1, None, axis=dim)
        rest = lambda a: lax.slice_in_dim(a, 1, None, axis=dim)
        head = lambda a: lax.slice_in_dim(a, 0, a.shape[dim] - 1, axis=dim)
        high = lax.ppermute(jnp.stack([first(correction), first(mobility)]), axis, backward)
        low = lax.ppermute(
            jnp.stack([last(correction), last(mobility), last(flag).astype(jnp.float32)]), axis, forward
        )
        press_next = jnp.concatenate([rest(correction), high[0]], axis=dim)
        mobil_next = jnp.concatenate([rest(mobility), high[1]], axis=dim)
        flux_high = jnp.where(flag == 1, mobility, mobil_next) * (correction - press_next)
        place = lax.broadcasted_iota(jnp.int32, correction.shape, dim)
        edge = (at == count - 1) & (place == correction.shape[dim] - 1)
        flux_high = jnp.where(edge, 0.0, flux_high)
        flux_edge = jnp.where(low[2] > 0.5, low[1], first(mobility)) * (low[0] - first(correction))
        flux_edge = jnp.where(at == 0, 0.0, flux_edge)
        flux_low = jnp.concatenate([flux_edge, head(flux_high)], axis=dim)
        return flux_high - flux_low

    balance = net("px", 2, flag_x, at_x, count_x) + net("py", 1, flag_y, at_y, count_y)
    return (correction, balance)


def solution(mesh):
    return jax.shard_map(
        shards,
        mesh=mesh,
        in_specs=(
            P(None, "py", "px"),
            P("px"),
            P("py"),
            P(),
            P(),
            P(None, "px"),
            P("py", None),
            P("py", None),
            P(None, "px"),
            P(None, "py", "px"),
            P(None, None, "py", "px"),
            P(),
        ),
        out_specs=(P(None, "py", "px"), P(None, "py", "px")),
        check_vma=False,
    )
```

```python
import jax
import jax.numpy as jnp
from jax import lax
from jax.experimental import pallas as pl
from jax.experimental.pallas import tpu as pltpu
from jax.sharding import PartitionSpec as P


def exchange(block, axis):
    count = lax.axis_size(axis)
    parts = [block]
    for k in range(1, count):
        parts.append(lax.ppermute(block, axis, [(s, s ^ k) for s in range(count)]))
    return parts


def in_exchange_order(matrix, axis):
    count = lax.axis_size(axis)
    own = lax.axis_index(axis)
    blocks = matrix.reshape(count, matrix.shape[0] // count, matrix.shape[1])
    return jnp.concatenate(
        [lax.dynamic_index_in_dim(blocks, own ^ k, 0, keepdims=False) for k in range(count)]
    )


def thomas_kernel(coupling_ref, shift_ref, ly_ref, lx_ref, rhs_ref, out_ref):
    layers = rhs_ref.shape[0]
    mode_sum = ly_ref[...] + lx_ref[...]
    ratios = []
    partial_values = []
    for layer_index in range(layers):
        diagonal = mode_sum + shift_ref[layer_index]
        if layer_index > 0:
            diagonal = diagonal + coupling_ref[layer_index - 1]
        if layer_index < layers - 1:
            diagonal = diagonal + coupling_ref[layer_index]
        if layer_index == 0:
            pivots = diagonal
            solved = rhs_ref[0] / pivots
        else:
            pivots = diagonal + coupling_ref[layer_index - 1] * ratios[-1]
            solved = (rhs_ref[layer_index] + coupling_ref[layer_index - 1] * partial_values[-1]) / pivots
        partial_values.append(solved)
        if layer_index < layers - 1:
            ratios.append(-coupling_ref[layer_index] / pivots)
    result = partial_values[layers - 1]
    out_ref[layers - 1] = result.astype(out_ref.dtype)
    for layer_index in range(layers - 2, -1, -1):
        result = partial_values[layer_index] - ratios[layer_index] * result
        out_ref[layer_index] = result.astype(out_ref.dtype)


def thomas_solve(rhs, lambda_x, lambda_y, coupling, layer_shift):
    layers, rows, modes = rhs.shape
    tile = min(rows, 256)
    smem = pl.BlockSpec(memory_space=pltpu.SMEM)
    return pl.pallas_call(
        thomas_kernel,
        grid=(rows // tile,),
        in_specs=[
            smem,
            smem,
            pl.BlockSpec((tile, 1), lambda j: (j, 0)),
            pl.BlockSpec((1, modes), lambda j: (0, 0)),
            pl.BlockSpec((layers, tile, modes), lambda j: (0, j, 0)),
        ],
        out_specs=pl.BlockSpec((layers, tile, modes), lambda j: (0, j, 0)),
        out_shape=jax.ShapeDtypeStruct(rhs.shape, jnp.bfloat16),
    )(coupling, layer_shift, lambda_y.reshape(rows, 1), lambda_x.reshape(1, modes), rhs)


def shards(
    residual,
    lambda_x,
    lambda_y,
    coupling,
    layer_shift,
    left_x,
    left_y,
    right_y,
    right_x,
    regime_code,
    upwind_flag,
    mobility_table,
):
    count_x = lax.axis_size("px")
    count_y = lax.axis_size("py")
    at_x = lax.axis_index("px")
    at_y = lax.axis_index("py")
    layers, height, width = residual.shape
    modes = left_x.shape[1] // count_y

    rounded = residual.astype(jnp.bfloat16)
    spectral_x = jnp.einsum(
        "zyx,xci->czyi",
        jnp.concatenate(exchange(rounded, "px"), axis=2),
        in_exchange_order(left_x, "px").reshape(-1, count_y, modes),
        preferred_element_type=jnp.float32,
    ).astype(jnp.bfloat16)
    pencil = lax.all_to_all(spectral_x, "py", 0, 0, tiled=True)
    high = lax.reduce_precision(lambda_y, exponent_bits=8, mantissa_bits=7)
    rest = lambda_y - high
    middle = lax.reduce_precision(rest, exponent_bits=8, mantissa_bits=7)
    low = lax.reduce_precision(rest - middle, exponent_bits=8, mantissa_bits=7)
    high, middle, low = (p.astype(jnp.bfloat16) for p in (high, middle, low))
    pieces = jnp.zeros((lambda_y.shape[0], 128), jnp.bfloat16)
    pieces = pieces.at[:, 0].set(high).at[:, 1].set(middle).at[:, 2].set(low)
    carried = lax.all_gather(jnp.concatenate([left_y, pieces], axis=1), "py", axis=0, tiled=True)
    columns = left_y.shape[1]
    spectral = jnp.einsum(
        "jsy,szyi->zji",
        carried[:, :columns].reshape(-1, count_y, height),
        pencil,
        preferred_element_type=jnp.float32,
    )
    own_x = lax.dynamic_slice_in_dim(lambda_x, at_y * modes, modes)
    got = carried[:, columns:columns + 3].astype(jnp.float32)
    all_y = got[:, 0] + (got[:, 1] + got[:, 2])
    solved = thomas_solve(spectral, own_x, all_y, coupling, layer_shift)
    back_pencil = jnp.einsum(
        "syj,zji->szyi",
        lax.all_gather(right_y, "py", axis=0, tiled=True).reshape(count_y, height, -1),
        solved,
        preferred_element_type=jnp.float32,
    ).astype(jnp.bfloat16)
    back_y = lax.all_to_all(back_pencil, "py", 0, 0, tiled=True)
    back_y = jnp.moveaxis(back_y, 0, 2).reshape(layers, height, -1)
    correction = jnp.einsum(
        "zyi,ix->zyx",
        lax.all_gather(back_y, "px", axis=2, tiled=True),
        right_x,
        preferred_element_type=jnp.float32,
    )

    mobility = jnp.zeros(regime_code.shape, jnp.float32)
    for regime in range(mobility_table.shape[0]):
        mobility = jnp.where(regime_code == regime, mobility_table[regime], mobility)
    flag_x = upwind_flag[0]
    flag_y = upwind_flag[1]

    def net(axis, dim, flag, at, count):
        forward = [(i, i + 1) for i in range(count - 1)]
        backward = [(i + 1, i) for i in range(count - 1)]
        first = lambda a: lax.slice_in_dim(a, 0, 1, axis=dim)
        last = lambda a: lax.slice_in_dim(a, a.shape[dim] - 1, None, axis=dim)
        rest = lambda a: lax.slice_in_dim(a, 1, None, axis=dim)
        head = lambda a: lax.slice_in_dim(a, 0, a.shape[dim] - 1, axis=dim)
        high = lax.ppermute(jnp.stack([first(correction), first(mobility)]), axis, backward)
        low = lax.ppermute(
            jnp.stack([last(correction), last(mobility), last(flag).astype(jnp.float32)]), axis, forward
        )
        press_next = jnp.concatenate([rest(correction), high[0]], axis=dim)
        mobil_next = jnp.concatenate([rest(mobility), high[1]], axis=dim)
        flux_high = jnp.where(flag == 1, mobility, mobil_next) * (correction - press_next)
        place = lax.broadcasted_iota(jnp.int32, correction.shape, dim)
        edge = (at == count - 1) & (place == correction.shape[dim] - 1)
        flux_high = jnp.where(edge, 0.0, flux_high)
        flux_edge = jnp.where(low[2] > 0.5, low[1], first(mobility)) * (low[0] - first(correction))
        flux_edge = jnp.where(at == 0, 0.0, flux_edge)
        flux_low = jnp.concatenate([flux_edge, head(flux_high)], axis=dim)
        return flux_high - flux_low

    balance = net("px", 2, flag_x, at_x, count_x) + net("py", 1, flag_y, at_y, count_y)
    return (correction, balance)


def solution(mesh):
    return jax.shard_map(
        shards,
        mesh=mesh,
        in_specs=(
            P(None, "py", "px"),
            P("px"),
            P("py"),
            P(),
            P(),
            P(None, "px"),
            P("py", None),
            P("py", None),
            P(None, "px"),
            P(None, "py", "px"),
            P(None, None, "py", "px"),
            P(),
        ),
        out_specs=(P(None, "py", "px"), P(None, "py", "px")),
        check_vma=False,
    )
```

```python
import jax
import jax.numpy as jnp
from jax import lax
from jax.experimental import pallas as pl
from jax.experimental.pallas import tpu as pltpu
from jax.sharding import PartitionSpec as P


def exchange(block, axis):
    count = lax.axis_size(axis)
    parts = [block]
    for k in range(1, count):
        parts.append(lax.ppermute(block, axis, [(s, s ^ k) for s in range(count)]))
    return parts


def in_exchange_order(matrix, axis):
    count = lax.axis_size(axis)
    own = lax.axis_index(axis)
    blocks = matrix.reshape(count, matrix.shape[0] // count, matrix.shape[1])
    return jnp.concatenate(
        [lax.dynamic_index_in_dim(blocks, own ^ k, 0, keepdims=False) for k in range(count)]
    )


def thomas_kernel(coupling_ref, shift_ref, ly_ref, lx_ref, rhs_ref, out_ref):
    layers = rhs_ref.shape[0]
    mode_sum = ly_ref[...] + lx_ref[...]
    ratios = []
    partial_values = []
    for layer_index in range(layers):
        diagonal = mode_sum + shift_ref[layer_index]
        if layer_index > 0:
            diagonal = diagonal + coupling_ref[layer_index - 1]
        if layer_index < layers - 1:
            diagonal = diagonal + coupling_ref[layer_index]
        if layer_index == 0:
            pivots = diagonal
            solved = rhs_ref[0] / pivots
        else:
            pivots = diagonal + coupling_ref[layer_index - 1] * ratios[-1]
            solved = (rhs_ref[layer_index] + coupling_ref[layer_index - 1] * partial_values[-1]) / pivots
        partial_values.append(solved)
        if layer_index < layers - 1:
            ratios.append(-coupling_ref[layer_index] / pivots)
    result = partial_values[layers - 1]
    out_ref[layers - 1] = result.astype(out_ref.dtype)
    for layer_index in range(layers - 2, -1, -1):
        result = partial_values[layer_index] - ratios[layer_index] * result
        out_ref[layer_index] = result.astype(out_ref.dtype)


def thomas_solve(rhs, lambda_x, lambda_y, coupling, layer_shift):
    layers, rows, modes = rhs.shape
    tile = min(rows, 256)
    smem = pl.BlockSpec(memory_space=pltpu.SMEM)
    return pl.pallas_call(
        thomas_kernel,
        grid=(rows // tile,),
        in_specs=[
            smem,
            smem,
            pl.BlockSpec((tile, 1), lambda j: (j, 0)),
            pl.BlockSpec((1, modes), lambda j: (0, 0)),
            pl.BlockSpec((layers, tile, modes), lambda j: (0, j, 0)),
        ],
        out_specs=pl.BlockSpec((layers, tile, modes), lambda j: (0, j, 0)),
        out_shape=jax.ShapeDtypeStruct(rhs.shape, jnp.bfloat16),
    )(coupling, layer_shift, lambda_y.reshape(rows, 1), lambda_x.reshape(1, modes), rhs)


def shards(
    residual,
    lambda_x,
    lambda_y,
    coupling,
    layer_shift,
    left_x,
    left_y,
    right_y,
    right_x,
    regime_code,
    upwind_flag,
    mobility_table,
):
    count_x = lax.axis_size("px")
    count_y = lax.axis_size("py")
    at_x = lax.axis_index("px")
    at_y = lax.axis_index("py")
    layers, height, width = residual.shape
    modes = left_x.shape[1] // count_y

    rounded = residual.astype(jnp.bfloat16)
    spectral_x = jnp.einsum(
        "zyx,xci->czyi",
        jnp.concatenate(exchange(rounded, "px"), axis=2),
        in_exchange_order(left_x, "px").reshape(-1, count_y, modes),
        preferred_element_type=jnp.float32,
    ).astype(jnp.bfloat16)
    pencil = lax.all_to_all(spectral_x, "py", 0, 0, tiled=True)
    high = lax.reduce_precision(lambda_y, exponent_bits=8, mantissa_bits=7)
    rest = lambda_y - high
    middle = lax.reduce_precision(rest, exponent_bits=8, mantissa_bits=7)
    low = lax.reduce_precision(rest - middle, exponent_bits=8, mantissa_bits=7)
    high, middle, low = (p.astype(jnp.bfloat16) for p in (high, middle, low))
    pieces = jnp.zeros((lambda_y.shape[0], 128), jnp.bfloat16)
    pieces = pieces.at[:, 0].set(high).at[:, 1].set(middle).at[:, 2].set(low)
    carried = lax.all_gather(jnp.concatenate([left_y, pieces], axis=1), "py", axis=0, tiled=True)
    columns = left_y.shape[1]
    spectral = jnp.einsum(
        "jsy,szyi->zji",
        carried[:, :columns].reshape(-1, count_y, height),
        pencil,
        preferred_element_type=jnp.float32,
    )
    own_x = lax.dynamic_slice_in_dim(lambda_x, at_y * modes, modes)
    got = carried[:, columns:columns + 3].astype(jnp.float32)
    all_y = got[:, 0] + (got[:, 1] + got[:, 2])
    solved = thomas_solve(spectral, own_x, all_y, coupling, layer_shift)
    right_all = lax.all_gather(right_y, "py", axis=0, tiled=True).reshape(count_y, height, -1)

    mobility = jnp.zeros(regime_code.shape, jnp.float32)
    for regime in range(mobility_table.shape[0]):
        mobility = jnp.where(regime_code == regime, mobility_table[regime], mobility)

    def back_half(solved, mobility, flag_x, flag_y):
        back_pencil = jnp.einsum(
            "syj,zji->szyi",
            right_all,
            solved,
            preferred_element_type=jnp.float32,
        ).astype(jnp.bfloat16)
        back_y = lax.all_to_all(back_pencil, "py", 0, 0, tiled=True)
        back_y = jnp.moveaxis(back_y, 0, 2).reshape(solved.shape[0], height, -1)
        correction = jnp.einsum(
            "zyi,ix->zyx",
            lax.all_gather(back_y, "px", axis=2, tiled=True),
            right_x,
            preferred_element_type=jnp.float32,
        )

        def net(axis, dim, flag, at, count):
            forward = [(i, i + 1) for i in range(count - 1)]
            backward = [(i + 1, i) for i in range(count - 1)]
            first = lambda a: lax.slice_in_dim(a, 0, 1, axis=dim)
            last = lambda a: lax.slice_in_dim(a, a.shape[dim] - 1, None, axis=dim)
            rest = lambda a: lax.slice_in_dim(a, 1, None, axis=dim)
            head = lambda a: lax.slice_in_dim(a, 0, a.shape[dim] - 1, axis=dim)
            high = lax.ppermute(jnp.stack([first(correction), first(mobility)]), axis, backward)
            low = lax.ppermute(
                jnp.stack([last(correction), last(mobility), last(flag).astype(jnp.float32)]), axis, forward
            )
            press_next = jnp.concatenate([rest(correction), high[0]], axis=dim)
            mobil_next = jnp.concatenate([rest(mobility), high[1]], axis=dim)
            flux_high = jnp.where(flag == 1, mobility, mobil_next) * (correction - press_next)
            place = lax.broadcasted_iota(jnp.int32, correction.shape, dim)
            edge = (at == count - 1) & (place == correction.shape[dim] - 1)
            flux_high = jnp.where(edge, 0.0, flux_high)
            flux_edge = jnp.where(low[2] > 0.5, low[1], first(mobility)) * (low[0] - first(correction))
            flux_edge = jnp.where(at == 0, 0.0, flux_edge)
            flux_low = jnp.concatenate([flux_edge, head(flux_high)], axis=dim)
            return flux_high - flux_low

        balance = net("px", 2, flag_x, at_x, count_x) + net("py", 1, flag_y, at_y, count_y)
        return correction, balance

    split = layers // 2
    parts = [
        back_half(solved[lo:hi], mobility[lo:hi], upwind_flag[0, lo:hi], upwind_flag[1, lo:hi])
        for lo, hi in ((0, split), (split, layers))
    ]
    correction = jnp.concatenate([p[0] for p in parts])
    balance = jnp.concatenate([p[1] for p in parts])
    return (correction, balance)


def solution(mesh):
    return jax.shard_map(
        shards,
        mesh=mesh,
        in_specs=(
            P(None, "py", "px"),
            P("px"),
            P("py"),
            P(),
            P(),
            P(None, "px"),
            P("py", None),
            P("py", None),
            P(None, "px"),
            P(None, "py", "px"),
            P(None, None, "py", "px"),
            P(),
        ),
        out_specs=(P(None, "py", "px"), P(None, "py", "px")),
        check_vma=False,
    )
```

```python
import jax
import jax.numpy as jnp
from jax import lax
from jax.experimental import pallas as pl
from jax.experimental.pallas import tpu as pltpu
from jax.sharding import PartitionSpec as P


def exchange(block, axis):
    count = lax.axis_size(axis)
    parts = [block]
    for k in range(1, count):
        parts.append(lax.ppermute(block, axis, [(s, s ^ k) for s in range(count)]))
    return parts


def in_exchange_order(matrix, axis):
    count = lax.axis_size(axis)
    own = lax.axis_index(axis)
    blocks = matrix.reshape(count, matrix.shape[0] // count, matrix.shape[1])
    return jnp.concatenate(
        [lax.dynamic_index_in_dim(blocks, own ^ k, 0, keepdims=False) for k in range(count)]
    )


def thomas_kernel(coupling_ref, shift_ref, ly_ref, lx_ref, rhs_ref, out_ref):
    layers = rhs_ref.shape[0]
    mode_sum = ly_ref[...] + lx_ref[...]
    ratios = []
    partial_values = []
    for layer_index in range(layers):
        diagonal = mode_sum + shift_ref[layer_index]
        if layer_index > 0:
            diagonal = diagonal + coupling_ref[layer_index - 1]
        if layer_index < layers - 1:
            diagonal = diagonal + coupling_ref[layer_index]
        if layer_index == 0:
            pivots = diagonal
            solved = rhs_ref[0] / pivots
        else:
            pivots = diagonal + coupling_ref[layer_index - 1] * ratios[-1]
            solved = (rhs_ref[layer_index] + coupling_ref[layer_index - 1] * partial_values[-1]) / pivots
        partial_values.append(solved)
        if layer_index < layers - 1:
            ratios.append(-coupling_ref[layer_index] / pivots)
    result = partial_values[layers - 1]
    out_ref[layers - 1] = result.astype(out_ref.dtype)
    for layer_index in range(layers - 2, -1, -1):
        result = partial_values[layer_index] - ratios[layer_index] * result
        out_ref[layer_index] = result.astype(out_ref.dtype)


def thomas_solve(rhs, lambda_x, lambda_y, coupling, layer_shift):
    layers, rows, modes = rhs.shape
    tile = min(rows, 256)
    smem = pl.BlockSpec(memory_space=pltpu.SMEM)
    return pl.pallas_call(
        thomas_kernel,
        grid=(rows // tile,),
        in_specs=[
            smem,
            smem,
            pl.BlockSpec((tile, 1), lambda j: (j, 0)),
            pl.BlockSpec((1, modes), lambda j: (0, 0)),
            pl.BlockSpec((layers, tile, modes), lambda j: (0, j, 0)),
        ],
        out_specs=pl.BlockSpec((layers, tile, modes), lambda j: (0, j, 0)),
        out_shape=jax.ShapeDtypeStruct(rhs.shape, jnp.bfloat16),
    )(coupling, layer_shift, lambda_y.reshape(rows, 1), lambda_x.reshape(1, modes), rhs)


def shards(
    residual,
    lambda_x,
    lambda_y,
    coupling,
    layer_shift,
    left_x,
    left_y,
    right_y,
    right_x,
    regime_code,
    upwind_flag,
    mobility_table,
):
    count_x = lax.axis_size("px")
    count_y = lax.axis_size("py")
    at_x = lax.axis_index("px")
    at_y = lax.axis_index("py")
    layers, height, width = residual.shape
    modes = left_x.shape[1] // count_y

    rounded = residual.astype(jnp.bfloat16)
    spectral_x = jnp.einsum(
        "zyx,xci->czyi",
        jnp.concatenate(exchange(rounded, "px"), axis=2),
        in_exchange_order(left_x, "px").reshape(-1, count_y, modes),
        preferred_element_type=jnp.float32,
    ).astype(jnp.bfloat16)
    pencil = lax.all_to_all(spectral_x, "py", 0, 0, tiled=True)
    high = lax.reduce_precision(lambda_y, exponent_bits=8, mantissa_bits=7)
    rest = lambda_y - high
    middle = lax.reduce_precision(rest, exponent_bits=8, mantissa_bits=7)
    low = lax.reduce_precision(rest - middle, exponent_bits=8, mantissa_bits=7)
    high, middle, low = (p.astype(jnp.bfloat16) for p in (high, middle, low))
    pieces = jnp.zeros((lambda_y.shape[0], 128), jnp.bfloat16)
    pieces = pieces.at[:, 0].set(high).at[:, 1].set(middle).at[:, 2].set(low)
    carried = lax.all_gather(jnp.concatenate([left_y, pieces], axis=1), "py", axis=0, tiled=True)
    columns = left_y.shape[1]
    spectral = jnp.einsum(
        "jsy,szyi->zji",
        carried[:, :columns].reshape(-1, count_y, height),
        pencil,
        preferred_element_type=jnp.float32,
    )
    own_x = lax.dynamic_slice_in_dim(lambda_x, at_y * modes, modes)
    got = carried[:, columns:columns + 3].astype(jnp.float32)
    all_y = got[:, 0] + (got[:, 1] + got[:, 2])
    solved = thomas_solve(spectral, own_x, all_y, coupling, layer_shift)
    back_pencil = jnp.einsum(
        "syj,zji->szyi",
        lax.all_gather(right_y, "py", axis=0, tiled=True).reshape(count_y, height, -1),
        solved,
        preferred_element_type=jnp.float32,
    ).astype(jnp.bfloat16)
    spread = jnp.broadcast_to(back_pencil[None], (count_x,) + back_pencil.shape)
    spread = spread.reshape((count_x * count_y,) + back_pencil.shape[1:])
    back_y = lax.all_to_all(spread, ("px", "py"), 0, 0, tiled=True)
    back_y = jnp.moveaxis(back_y, 0, 2).reshape(layers, height, -1)
    correction = jnp.einsum(
        "zyi,ix->zyx",
        back_y,
        right_x,
        preferred_element_type=jnp.float32,
    )

    mobility = jnp.zeros(regime_code.shape, jnp.float32)
    for regime in range(mobility_table.shape[0]):
        mobility = jnp.where(regime_code == regime, mobility_table[regime], mobility)
    flag_x = upwind_flag[0]
    flag_y = upwind_flag[1]

    def net(axis, dim, flag, at, count):
        forward = [(i, i + 1) for i in range(count - 1)]
        backward = [(i + 1, i) for i in range(count - 1)]
        first = lambda a: lax.slice_in_dim(a, 0, 1, axis=dim)
        last = lambda a: lax.slice_in_dim(a, a.shape[dim] - 1, None, axis=dim)
        rest = lambda a: lax.slice_in_dim(a, 1, None, axis=dim)
        head = lambda a: lax.slice_in_dim(a, 0, a.shape[dim] - 1, axis=dim)
        high = lax.ppermute(jnp.stack([first(correction), first(mobility)]), axis, backward)
        low = lax.ppermute(
            jnp.stack([last(correction), last(mobility), last(flag).astype(jnp.float32)]), axis, forward
        )
        press_next = jnp.concatenate([rest(correction), high[0]], axis=dim)
        mobil_next = jnp.concatenate([rest(mobility), high[1]], axis=dim)
        flux_high = jnp.where(flag == 1, mobility, mobil_next) * (correction - press_next)
        place = lax.broadcasted_iota(jnp.int32, correction.shape, dim)
        edge = (at == count - 1) & (place == correction.shape[dim] - 1)
        flux_high = jnp.where(edge, 0.0, flux_high)
        flux_edge = jnp.where(low[2] > 0.5, low[1], first(mobility)) * (low[0] - first(correction))
        flux_edge = jnp.where(at == 0, 0.0, flux_edge)
        flux_low = jnp.concatenate([flux_edge, head(flux_high)], axis=dim)
        return flux_high - flux_low

    balance = net("px", 2, flag_x, at_x, count_x) + net("py", 1, flag_y, at_y, count_y)
    return (correction, balance)


def solution(mesh):
    return jax.shard_map(
        shards,
        mesh=mesh,
        in_specs=(
            P(None, "py", "px"),
            P("px"),
            P("py"),
            P(),
            P(),
            P(None, "px"),
            P("py", None),
            P("py", None),
            P(None, "px"),
            P(None, "py", "px"),
            P(None, None, "py", "px"),
            P(),
        ),
        out_specs=(P(None, "py", "px"), P(None, "py", "px")),
        check_vma=False,
    )
```

```python
import jax
import jax.numpy as jnp
from jax import lax
from jax.experimental import pallas as pl
from jax.experimental.pallas import tpu as pltpu
from jax.sharding import PartitionSpec as P


def exchange(block, axis):
    count = lax.axis_size(axis)
    parts = [block]
    for k in range(1, count):
        parts.append(lax.ppermute(block, axis, [(s, s ^ k) for s in range(count)]))
    return parts


def in_exchange_order(matrix, axis):
    count = lax.axis_size(axis)
    own = lax.axis_index(axis)
    blocks = matrix.reshape(count, matrix.shape[0] // count, matrix.shape[1])
    return jnp.concatenate(
        [lax.dynamic_index_in_dim(blocks, own ^ k, 0, keepdims=False) for k in range(count)]
    )


def thomas_kernel(coupling_ref, shift_ref, ly_ref, lx_ref, rhs_ref, out_ref):
    layers = rhs_ref.shape[0]
    mode_sum = ly_ref[...] + lx_ref[...]
    ratios = []
    partial_values = []
    for layer_index in range(layers):
        diagonal = mode_sum + shift_ref[layer_index]
        if layer_index > 0:
            diagonal = diagonal + coupling_ref[layer_index - 1]
        if layer_index < layers - 1:
            diagonal = diagonal + coupling_ref[layer_index]
        if layer_index == 0:
            pivots = diagonal
            solved = rhs_ref[0] / pivots
        else:
            pivots = diagonal + coupling_ref[layer_index - 1] * ratios[-1]
            solved = (rhs_ref[layer_index] + coupling_ref[layer_index - 1] * partial_values[-1]) / pivots
        partial_values.append(solved)
        if layer_index < layers - 1:
            ratios.append(-coupling_ref[layer_index] / pivots)
    result = partial_values[layers - 1]
    out_ref[layers - 1] = result.astype(out_ref.dtype)
    for layer_index in range(layers - 2, -1, -1):
        result = partial_values[layer_index] - ratios[layer_index] * result
        out_ref[layer_index] = result.astype(out_ref.dtype)


def thomas_solve(rhs, lambda_x, lambda_y, coupling, layer_shift):
    layers, rows, modes = rhs.shape
    tile = min(rows, 256)
    smem = pl.BlockSpec(memory_space=pltpu.SMEM)
    return pl.pallas_call(
        thomas_kernel,
        grid=(rows // tile,),
        in_specs=[
            smem,
            smem,
            pl.BlockSpec((tile, 1), lambda j: (j, 0)),
            pl.BlockSpec((1, modes), lambda j: (0, 0)),
            pl.BlockSpec((layers, tile, modes), lambda j: (0, j, 0)),
        ],
        out_specs=pl.BlockSpec((layers, tile, modes), lambda j: (0, j, 0)),
        out_shape=jax.ShapeDtypeStruct(rhs.shape, jnp.bfloat16),
    )(coupling, layer_shift, lambda_y.reshape(rows, 1), lambda_x.reshape(1, modes), rhs)


def shards(
    residual,
    lambda_x,
    lambda_y,
    coupling,
    layer_shift,
    left_x,
    left_y,
    right_y,
    right_x,
    regime_code,
    upwind_flag,
    mobility_table,
):
    count_x = lax.axis_size("px")
    count_y = lax.axis_size("py")
    at_x = lax.axis_index("px")
    at_y = lax.axis_index("py")
    layers, height, width = residual.shape
    modes = left_x.shape[1] // count_y

    rounded = residual.astype(jnp.bfloat16)
    spectral_x = jnp.einsum(
        "zyx,xci->czyi",
        jnp.concatenate(exchange(rounded, "px"), axis=2),
        in_exchange_order(left_x, "px").reshape(-1, count_y, modes),
        preferred_element_type=jnp.float32,
    ).astype(jnp.bfloat16)
    pencil = lax.all_to_all(spectral_x, "py", 0, 0, tiled=True)
    high = lax.reduce_precision(lambda_y, exponent_bits=8, mantissa_bits=7)
    rest = lambda_y - high
    middle = lax.reduce_precision(rest, exponent_bits=8, mantissa_bits=7)
    low = lax.reduce_precision(rest - middle, exponent_bits=8, mantissa_bits=7)
    high, middle, low = (p.astype(jnp.bfloat16) for p in (high, middle, low))
    pieces = jnp.zeros((lambda_y.shape[0], 128), jnp.bfloat16)
    pieces = pieces.at[:, 0].set(high).at[:, 1].set(middle).at[:, 2].set(low)
    carried = lax.all_gather(jnp.concatenate([left_y, pieces], axis=1), "py", axis=0, tiled=True)
    columns = left_y.shape[1]
    spectral = jnp.einsum(
        "jsy,szyi->zji",
        carried[:, :columns].reshape(-1, count_y, height),
        pencil,
        preferred_element_type=jnp.float32,
    )
    own_x = lax.dynamic_slice_in_dim(lambda_x, at_y * modes, modes)
    got = carried[:, columns:columns + 3].astype(jnp.float32)
    all_y = got[:, 0] + (got[:, 1] + got[:, 2])
    solved = thomas_solve(spectral, own_x, all_y, coupling, layer_shift)
    right_all = lax.all_gather(right_y, "py", axis=0, tiled=True)
    rows = jnp.clip(
        jnp.arange(count_y)[:, None] * height - 1 + jnp.arange(height + 2)[None, :], 0, right_all.shape[0] - 1
    )
    back_pencil = jnp.einsum(
        "syj,zji->szyi",
        jnp.take(right_all, rows, axis=0),
        solved,
        preferred_element_type=jnp.float32,
    ).astype(jnp.bfloat16)
    back_y = lax.all_to_all(back_pencil, "py", 0, 0, tiled=True)
    back_y = jnp.moveaxis(back_y, 0, 2).reshape(layers, height + 2, -1)

    forward_x = [(i, i + 1) for i in range(count_x - 1)]
    backward_x = [(i + 1, i) for i in range(count_x - 1)]
    forward_y = [(i, i + 1) for i in range(count_y - 1)]
    backward_y = [(i + 1, i) for i in range(count_y - 1)]
    right_ext = jnp.concatenate(
        [
            lax.ppermute(right_x[:, -1:], "px", forward_x),
            right_x,
            lax.ppermute(right_x[:, :1], "px", backward_x),
        ],
        axis=1,
    )
    extended = jnp.einsum(
        "zyi,ix->zyx",
        lax.all_gather(back_y, "px", axis=2, tiled=True),
        right_ext,
        preferred_element_type=jnp.float32,
    )
    correction = extended[:, 1:-1, 1:-1]

    mobility = jnp.zeros(regime_code.shape, jnp.float32)
    for regime in range(mobility_table.shape[0]):
        mobility = jnp.where(regime_code == regime, mobility_table[regime], mobility)
    flag_x = upwind_flag[0].astype(jnp.float32)
    flag_y = upwind_flag[1].astype(jnp.float32)

    left = lax.ppermute(jnp.stack([mobility[:, :, -1:], flag_x[:, :, -1:]]), "px", forward_x)
    right = lax.ppermute(mobility[:, :, :1], "px", backward_x)
    up = lax.ppermute(jnp.stack([mobility[:, -1:, :], flag_y[:, -1:, :]]), "py", forward_y)
    down = lax.ppermute(mobility[:, :1, :], "py", backward_y)

    def net(press, mobil, flag, at, count, dim):
        size = press.shape[dim] - 2
        lo = lambda a: lax.slice_in_dim(a, 0, a.shape[dim] - 1, axis=dim)
        hi = lambda a: lax.slice_in_dim(a, 1, None, axis=dim)
        flux = jnp.where(flag == 1.0, lo(mobil), hi(mobil)) * (lo(press) - hi(press))
        face = lax.broadcasted_iota(jnp.int32, flux.shape, dim) + at * size - 1
        flux = jnp.where((face >= 0) & (face <= size * count - 2), flux, 0.0)
        return hi(flux) - lo(flux)

    net_x = net(
        extended[:, 1:-1, :],
        jnp.concatenate([left[0], mobility, right], axis=2),
        jnp.concatenate([left[1], flag_x], axis=2),
        at_x,
        count_x,
        2,
    )
    net_y = net(
        extended[:, :, 1:-1],
        jnp.concatenate([up[0], mobility, down], axis=1),
        jnp.concatenate([up[1], flag_y], axis=1),
        at_y,
        count_y,
        1,
    )
    balance = net_x + net_y
    return (correction, balance)


def solution(mesh):
    return jax.shard_map(
        shards,
        mesh=mesh,
        in_specs=(
            P(None, "py", "px"),
            P("px"),
            P("py"),
            P(),
            P(),
            P(None, "px"),
            P("py", None),
            P("py", None),
            P(None, "px"),
            P(None, "py", "px"),
            P(None, None, "py", "px"),
            P(),
        ),
        out_specs=(P(None, "py", "px"), P(None, "py", "px")),
        check_vma=False,
    )
```

```python
import jax
import jax.numpy as jnp
from jax import lax
from jax.experimental import pallas as pl
from jax.experimental.pallas import tpu as pltpu
from jax.sharding import PartitionSpec as P


def exchange(block, axis):
    count = lax.axis_size(axis)
    parts = [block]
    for k in range(1, count):
        parts.append(lax.ppermute(block, axis, [(s, s ^ k) for s in range(count)]))
    return parts


def in_exchange_order(matrix, axis):
    count = lax.axis_size(axis)
    own = lax.axis_index(axis)
    blocks = matrix.reshape(count, matrix.shape[0] // count, matrix.shape[1])
    return jnp.concatenate(
        [lax.dynamic_index_in_dim(blocks, own ^ k, 0, keepdims=False) for k in range(count)]
    )


def thomas_kernel(coupling_ref, shift_ref, ly_ref, lx_ref, rhs_ref, out_ref):
    layers = rhs_ref.shape[0]
    mode_sum = ly_ref[...] + lx_ref[...]
    ratios = []
    partial_values = []
    for layer_index in range(layers):
        diagonal = mode_sum + shift_ref[layer_index]
        if layer_index > 0:
            diagonal = diagonal + coupling_ref[layer_index - 1]
        if layer_index < layers - 1:
            diagonal = diagonal + coupling_ref[layer_index]
        if layer_index == 0:
            pivots = diagonal
            solved = rhs_ref[0] / pivots
        else:
            pivots = diagonal + coupling_ref[layer_index - 1] * ratios[-1]
            solved = (rhs_ref[layer_index] + coupling_ref[layer_index - 1] * partial_values[-1]) / pivots
        partial_values.append(solved)
        if layer_index < layers - 1:
            ratios.append(-coupling_ref[layer_index] / pivots)
    result = partial_values[layers - 1]
    out_ref[layers - 1] = result.astype(out_ref.dtype)
    for layer_index in range(layers - 2, -1, -1):
        result = partial_values[layer_index] - ratios[layer_index] * result
        out_ref[layer_index] = result.astype(out_ref.dtype)


def thomas_solve(rhs, lambda_x, lambda_y, coupling, layer_shift):
    layers, rows, modes = rhs.shape
    tile = min(rows, 256)
    smem = pl.BlockSpec(memory_space=pltpu.SMEM)
    return pl.pallas_call(
        thomas_kernel,
        grid=(rows // tile,),
        in_specs=[
            smem,
            smem,
            pl.BlockSpec((tile, 1), lambda j: (j, 0)),
            pl.BlockSpec((1, modes), lambda j: (0, 0)),
            pl.BlockSpec((layers, tile, modes), lambda j: (0, j, 0)),
        ],
        out_specs=pl.BlockSpec((layers, tile, modes), lambda j: (0, j, 0)),
        out_shape=jax.ShapeDtypeStruct(rhs.shape, jnp.bfloat16),
    )(coupling, layer_shift, lambda_y.reshape(rows, 1), lambda_x.reshape(1, modes), rhs)


def shards(
    residual,
    lambda_x,
    lambda_y,
    coupling,
    layer_shift,
    left_x,
    left_y,
    right_y,
    right_x,
    regime_code,
    upwind_flag,
    mobility_table,
):
    count_x = lax.axis_size("px")
    count_y = lax.axis_size("py")
    at_x = lax.axis_index("px")
    at_y = lax.axis_index("py")
    layers, height, width = residual.shape
    modes = left_x.shape[1] // count_y

    rounded = residual.astype(jnp.bfloat16)
    spectral_x = jnp.einsum(
        "zyx,xci->czyi",
        jnp.concatenate(exchange(rounded, "px"), axis=2),
        in_exchange_order(left_x, "px").reshape(-1, count_y, modes),
        preferred_element_type=jnp.float32,
    ).astype(jnp.bfloat16)
    pencil = lax.all_to_all(spectral_x, "py", 0, 0, tiled=True)
    high = lax.reduce_precision(lambda_y, exponent_bits=8, mantissa_bits=7)
    rest = lambda_y - high
    middle = lax.reduce_precision(rest, exponent_bits=8, mantissa_bits=7)
    low = lax.reduce_precision(rest - middle, exponent_bits=8, mantissa_bits=7)
    high, middle, low = (p.astype(jnp.bfloat16) for p in (high, middle, low))
    pieces = jnp.zeros((lambda_y.shape[0], 128), jnp.bfloat16)
    pieces = pieces.at[:, 0].set(high).at[:, 1].set(middle).at[:, 2].set(low)
    carried = lax.all_gather(jnp.concatenate([left_y, pieces], axis=1), "py", axis=0, tiled=True)
    columns = left_y.shape[1]
    spectral = jnp.einsum(
        "jsy,szyi->zji",
        carried[:, :columns].reshape(-1, count_y, height),
        pencil,
        preferred_element_type=jnp.float32,
    )
    own_x = lax.dynamic_slice_in_dim(lambda_x, at_y * modes, modes)
    got = carried[:, columns:columns + 3].astype(jnp.float32)
    all_y = got[:, 0] + (got[:, 1] + got[:, 2])
    solved = thomas_solve(spectral, own_x, all_y, coupling, layer_shift)
    back_pencil = jnp.einsum(
        "syj,zji->szyi",
        lax.all_gather(right_y, "py", axis=0, tiled=True).reshape(count_y, height, -1),
        solved,
        preferred_element_type=jnp.float32,
    ).astype(jnp.bfloat16)
    back_y = lax.all_to_all(back_pencil, "py", 0, 0, tiled=True)
    back_y = jnp.moveaxis(back_y, 0, 2).reshape(layers, height, -1)

    forward_x = [(i, i + 1) for i in range(count_x - 1)]
    backward_x = [(i + 1, i) for i in range(count_x - 1)]
    forward_y = [(i, i + 1) for i in range(count_y - 1)]
    backward_y = [(i + 1, i) for i in range(count_y - 1)]
    right_ext = jnp.concatenate(
        [
            lax.ppermute(right_x[:, -1:], "px", forward_x),
            right_x,
            lax.ppermute(right_x[:, :1], "px", backward_x),
        ],
        axis=1,
    )
    extended = jnp.einsum(
        "zyi,ix->zyx",
        lax.all_gather(back_y, "px", axis=2, tiled=True),
        right_ext,
        preferred_element_type=jnp.float32,
    )
    correction = extended[:, :, 1:-1]

    mobility = jnp.zeros(regime_code.shape, jnp.float32)
    for regime in range(mobility_table.shape[0]):
        mobility = jnp.where(regime_code == regime, mobility_table[regime], mobility)
    flag_x = upwind_flag[0].astype(jnp.float32)
    flag_y = upwind_flag[1].astype(jnp.float32)

    left = lax.ppermute(jnp.stack([mobility[:, :, -1:], flag_x[:, :, -1:]]), "px", forward_x)
    right = lax.ppermute(mobility[:, :, :1], "px", backward_x)
    up = lax.ppermute(jnp.stack([mobility[:, -1:, :], flag_y[:, -1:, :]]), "py", forward_y)
    down = lax.ppermute(mobility[:, :1, :], "py", backward_y)

    def net(press, mobil, flag, at, count, dim):
        size = press.shape[dim] - 2
        lo = lambda a: lax.slice_in_dim(a, 0, a.shape[dim] - 1, axis=dim)
        hi = lambda a: lax.slice_in_dim(a, 1, None, axis=dim)
        flux = jnp.where(flag == 1.0, lo(mobil), hi(mobil)) * (lo(press) - hi(press))
        face = lax.broadcasted_iota(jnp.int32, flux.shape, dim) + at * size - 1
        flux = jnp.where((face >= 0) & (face <= size * count - 2), flux, 0.0)
        return hi(flux) - lo(flux)

    above = lax.ppermute(correction[:, -1:, :], "py", forward_y)
    below = lax.ppermute(correction[:, :1, :], "py", backward_y)
    net_x = net(
        extended,
        jnp.concatenate([left[0], mobility, right], axis=2),
        jnp.concatenate([left[1], flag_x], axis=2),
        at_x,
        count_x,
        2,
    )
    net_y = net(
        jnp.concatenate([above, correction, below], axis=1),
        jnp.concatenate([up[0], mobility, down], axis=1),
        jnp.concatenate([up[1], flag_y], axis=1),
        at_y,
        count_y,
        1,
    )
    balance = net_x + net_y
    return (correction, balance)


def solution(mesh):
    return jax.shard_map(
        shards,
        mesh=mesh,
        in_specs=(
            P(None, "py", "px"),
            P("px"),
            P("py"),
            P(),
            P(),
            P(None, "px"),
            P("py", None),
            P("py", None),
            P(None, "px"),
            P(None, "py", "px"),
            P(None, None, "py", "px"),
            P(),
        ),
        out_specs=(P(None, "py", "px"), P(None, "py", "px")),
        check_vma=False,
    )
```

```python
import jax
import jax.numpy as jnp
from jax import lax
from jax.experimental import pallas as pl
from jax.experimental.pallas import tpu as pltpu
from jax.sharding import PartitionSpec as P


def exchange(block, axis):
    count = lax.axis_size(axis)
    parts = [block]
    for k in range(1, count):
        parts.append(lax.ppermute(block, axis, [(s, s ^ k) for s in range(count)]))
    return parts


def in_exchange_order(matrix, axis):
    count = lax.axis_size(axis)
    own = lax.axis_index(axis)
    blocks = matrix.reshape(count, matrix.shape[0] // count, matrix.shape[1])
    return jnp.concatenate(
        [lax.dynamic_index_in_dim(blocks, own ^ k, 0, keepdims=False) for k in range(count)]
    )


def thomas_kernel(coupling_ref, shift_ref, ly_ref, lx_ref, rhs_ref, out_ref):
    layers = rhs_ref.shape[0]
    mode_sum = ly_ref[...] + lx_ref[...]
    ratios = []
    partial_values = []
    for layer_index in range(layers):
        diagonal = mode_sum + shift_ref[layer_index]
        if layer_index > 0:
            diagonal = diagonal + coupling_ref[layer_index - 1]
        if layer_index < layers - 1:
            diagonal = diagonal + coupling_ref[layer_index]
        if layer_index == 0:
            pivots = diagonal
            solved = rhs_ref[0] / pivots
        else:
            pivots = diagonal + coupling_ref[layer_index - 1] * ratios[-1]
            solved = (rhs_ref[layer_index] + coupling_ref[layer_index - 1] * partial_values[-1]) / pivots
        partial_values.append(solved)
        if layer_index < layers - 1:
            ratios.append(-coupling_ref[layer_index] / pivots)
    result = partial_values[layers - 1]
    out_ref[layers - 1] = result.astype(out_ref.dtype)
    for layer_index in range(layers - 2, -1, -1):
        result = partial_values[layer_index] - ratios[layer_index] * result
        out_ref[layer_index] = result.astype(out_ref.dtype)


def thomas_solve(rhs, lambda_x, lambda_y, coupling, layer_shift):
    layers, modes, rows = rhs.shape
    tile = min(rows, 512)
    smem = pl.BlockSpec(memory_space=pltpu.SMEM)
    return pl.pallas_call(
        thomas_kernel,
        grid=(rows // tile,),
        in_specs=[
            smem,
            smem,
            pl.BlockSpec((1, tile), lambda j: (0, j)),
            pl.BlockSpec((modes, 1), lambda j: (0, 0)),
            pl.BlockSpec((layers, modes, tile), lambda j: (0, 0, j)),
        ],
        out_specs=pl.BlockSpec((layers, modes, tile), lambda j: (0, 0, j)),
        out_shape=jax.ShapeDtypeStruct(rhs.shape, jnp.bfloat16),
    )(coupling, layer_shift, lambda_y.reshape(1, rows), lambda_x.reshape(modes, 1), rhs)


def shards(
    residual,
    lambda_x,
    lambda_y,
    coupling,
    layer_shift,
    left_x,
    left_y,
    right_y,
    right_x,
    regime_code,
    upwind_flag,
    mobility_table,
):
    count_x = lax.axis_size("px")
    count_y = lax.axis_size("py")
    at_x = lax.axis_index("px")
    at_y = lax.axis_index("py")
    layers, height, width = residual.shape
    modes = left_x.shape[1] // count_y

    rounded = residual.astype(jnp.bfloat16)
    spectral_x = jnp.einsum(
        "zyx,xci->czyi",
        jnp.concatenate(exchange(rounded, "px"), axis=2),
        in_exchange_order(left_x, "px").reshape(-1, count_y, modes),
        preferred_element_type=jnp.float32,
    ).astype(jnp.bfloat16)
    pencil = lax.all_to_all(spectral_x, "py", 0, 0, tiled=True)
    high = lax.reduce_precision(lambda_y, exponent_bits=8, mantissa_bits=7)
    rest = lambda_y - high
    middle = lax.reduce_precision(rest, exponent_bits=8, mantissa_bits=7)
    low = lax.reduce_precision(rest - middle, exponent_bits=8, mantissa_bits=7)
    high, middle, low = (p.astype(jnp.bfloat16) for p in (high, middle, low))
    pieces = jnp.zeros((lambda_y.shape[0], 128), jnp.bfloat16)
    pieces = pieces.at[:, 0].set(high).at[:, 1].set(middle).at[:, 2].set(low)
    carried = lax.all_gather(jnp.concatenate([left_y, pieces], axis=1), "py", axis=0, tiled=True)
    columns = left_y.shape[1]
    flat = jnp.transpose(pencil, (1, 3, 0, 2)).reshape(layers * modes, -1)
    spectral = jnp.einsum(
        "ny,jy->nj",
        flat,
        carried[:, :columns],
        preferred_element_type=jnp.float32,
    ).reshape(layers, modes, -1)
    own_x = lax.dynamic_slice_in_dim(lambda_x, at_y * modes, modes)
    got = carried[:, columns:columns + 3].astype(jnp.float32)
    all_y = got[:, 0] + (got[:, 1] + got[:, 2])
    solved = thomas_solve(spectral, own_x, all_y, coupling, layer_shift)
    back_flat = jnp.einsum(
        "nj,yj->ny",
        solved.reshape(layers * modes, -1),
        lax.all_gather(right_y, "py", axis=0, tiled=True),
        preferred_element_type=jnp.float32,
    ).astype(jnp.bfloat16)
    back_pencil = jnp.transpose(back_flat.reshape(layers, modes, count_y, height), (2, 0, 3, 1))
    back_y = lax.all_to_all(back_pencil, "py", 0, 0, tiled=True)
    back_y = jnp.moveaxis(back_y, 0, 2).reshape(layers, height, -1)
    correction = jnp.einsum(
        "zyi,ix->zyx",
        lax.all_gather(back_y, "px", axis=2, tiled=True),
        right_x,
        preferred_element_type=jnp.float32,
    )

    mobility = jnp.zeros(regime_code.shape, jnp.float32)
    for regime in range(mobility_table.shape[0]):
        mobility = jnp.where(regime_code == regime, mobility_table[regime], mobility)
    flag_x = upwind_flag[0]
    flag_y = upwind_flag[1]

    def net(axis, dim, flag, at, count):
        forward = [(i, i + 1) for i in range(count - 1)]
        backward = [(i + 1, i) for i in range(count - 1)]
        first = lambda a: lax.slice_in_dim(a, 0, 1, axis=dim)
        last = lambda a: lax.slice_in_dim(a, a.shape[dim] - 1, None, axis=dim)
        rest = lambda a: lax.slice_in_dim(a, 1, None, axis=dim)
        head = lambda a: lax.slice_in_dim(a, 0, a.shape[dim] - 1, axis=dim)
        high = lax.ppermute(jnp.stack([first(correction), first(mobility)]), axis, backward)
        low = lax.ppermute(
            jnp.stack([last(correction), last(mobility), last(flag).astype(jnp.float32)]), axis, forward
        )
        press_next = jnp.concatenate([rest(correction), high[0]], axis=dim)
        mobil_next = jnp.concatenate([rest(mobility), high[1]], axis=dim)
        flux_high = jnp.where(flag == 1, mobility, mobil_next) * (correction - press_next)
        place = lax.broadcasted_iota(jnp.int32, correction.shape, dim)
        edge = (at == count - 1) & (place == correction.shape[dim] - 1)
        flux_high = jnp.where(edge, 0.0, flux_high)
        flux_edge = jnp.where(low[2] > 0.5, low[1], first(mobility)) * (low[0] - first(correction))
        flux_edge = jnp.where(at == 0, 0.0, flux_edge)
        flux_low = jnp.concatenate([flux_edge, head(flux_high)], axis=dim)
        return flux_high - flux_low

    balance = net("px", 2, flag_x, at_x, count_x) + net("py", 1, flag_y, at_y, count_y)
    return (correction, balance)


def solution(mesh):
    return jax.shard_map(
        shards,
        mesh=mesh,
        in_specs=(
            P(None, "py", "px"),
            P("px"),
            P("py"),
            P(),
            P(),
            P(None, "px"),
            P("py", None),
            P("py", None),
            P(None, "px"),
            P(None, "py", "px"),
            P(None, None, "py", "px"),
            P(),
        ),
        out_specs=(P(None, "py", "px"), P(None, "py", "px")),
        check_vma=False,
    )
```

```python
import jax
import jax.numpy as jnp
from jax import lax
from jax.experimental import pallas as pl
from jax.experimental.pallas import tpu as pltpu
from jax.sharding import PartitionSpec as P


def exchange(block, axis):
    count = lax.axis_size(axis)
    parts = [block]
    for k in range(1, count):
        parts.append(lax.ppermute(block, axis, [(s, s ^ k) for s in range(count)]))
    return parts


def in_exchange_order(matrix, axis):
    count = lax.axis_size(axis)
    own = lax.axis_index(axis)
    blocks = matrix.reshape(count, matrix.shape[0] // count, matrix.shape[1])
    return jnp.concatenate(
        [lax.dynamic_index_in_dim(blocks, own ^ k, 0, keepdims=False) for k in range(count)]
    )


def thomas_kernel(coupling_ref, shift_ref, ly_ref, lx_ref, rhs_ref, out_ref):
    layers = rhs_ref.shape[0]
    mode_sum = ly_ref[...] + lx_ref[...]
    ratios = []
    partial_values = []
    for layer_index in range(layers):
        diagonal = mode_sum + shift_ref[layer_index]
        if layer_index > 0:
            diagonal = diagonal + coupling_ref[layer_index - 1]
        if layer_index < layers - 1:
            diagonal = diagonal + coupling_ref[layer_index]
        if layer_index == 0:
            pivots = diagonal
            solved = rhs_ref[0] / pivots
        else:
            pivots = diagonal + coupling_ref[layer_index - 1] * ratios[-1]
            solved = (rhs_ref[layer_index] + coupling_ref[layer_index - 1] * partial_values[-1]) / pivots
        partial_values.append(solved)
        if layer_index < layers - 1:
            ratios.append(-coupling_ref[layer_index] / pivots)
    result = partial_values[layers - 1]
    out_ref[layers - 1] = result.astype(out_ref.dtype)
    for layer_index in range(layers - 2, -1, -1):
        result = partial_values[layer_index] - ratios[layer_index] * result
        out_ref[layer_index] = result.astype(out_ref.dtype)


def thomas_solve(rhs, lambda_x, lambda_y, coupling, layer_shift):
    layers, modes, rows = rhs.shape
    tile = min(rows, 512)
    smem = pl.BlockSpec(memory_space=pltpu.SMEM)
    return pl.pallas_call(
        thomas_kernel,
        grid=(rows // tile,),
        in_specs=[
            smem,
            smem,
            pl.BlockSpec((1, tile), lambda j: (0, j)),
            pl.BlockSpec((modes, 1), lambda j: (0, 0)),
            pl.BlockSpec((layers, modes, tile), lambda j: (0, 0, j)),
        ],
        out_specs=pl.BlockSpec((layers, modes, tile), lambda j: (0, 0, j)),
        out_shape=jax.ShapeDtypeStruct(rhs.shape, jnp.bfloat16),
    )(coupling, layer_shift, lambda_y.reshape(1, rows), lambda_x.reshape(modes, 1), rhs)


def shards(
    residual,
    lambda_x,
    lambda_y,
    coupling,
    layer_shift,
    left_x,
    left_y,
    right_y,
    right_x,
    regime_code,
    upwind_flag,
    mobility_table,
):
    count_x = lax.axis_size("px")
    count_y = lax.axis_size("py")
    at_x = lax.axis_index("px")
    at_y = lax.axis_index("py")
    layers, height, width = residual.shape
    modes = left_x.shape[1] // count_y

    rounded = residual.astype(jnp.bfloat16)
    spectral_x = jnp.einsum(
        "zyx,xci->czyi",
        jnp.concatenate(exchange(rounded, "px"), axis=2),
        in_exchange_order(left_x, "px").reshape(-1, count_y, modes),
        preferred_element_type=jnp.float32,
    ).astype(jnp.bfloat16)
    pencil = lax.all_to_all(spectral_x, "py", 0, 0, tiled=True)
    high = lax.reduce_precision(lambda_y, exponent_bits=8, mantissa_bits=7)
    rest = lambda_y - high
    middle = lax.reduce_precision(rest, exponent_bits=8, mantissa_bits=7)
    low = lax.reduce_precision(rest - middle, exponent_bits=8, mantissa_bits=7)
    high, middle, low = (p.astype(jnp.bfloat16) for p in (high, middle, low))
    pieces = jnp.zeros((lambda_y.shape[0], 128), jnp.bfloat16)
    pieces = pieces.at[:, 0].set(high).at[:, 1].set(middle).at[:, 2].set(low)
    carried = lax.all_gather(jnp.concatenate([left_y, pieces], axis=1), "py", axis=0, tiled=True)
    columns = left_y.shape[1]
    flat = jnp.transpose(pencil, (1, 3, 0, 2)).reshape(layers * modes, -1)
    spectral = jnp.einsum(
        "ny,jy->nj",
        flat,
        carried[:, :columns],
        preferred_element_type=jnp.float32,
    ).reshape(layers, modes, -1)
    own_x = lax.dynamic_slice_in_dim(lambda_x, at_y * modes, modes)
    got = carried[:, columns:columns + 3].astype(jnp.float32)
    all_y = got[:, 0] + (got[:, 1] + got[:, 2])
    solved = thomas_solve(spectral, own_x, all_y, coupling, layer_shift)
    back_flat = jnp.einsum(
        "nj,yj->ny",
        solved.reshape(layers * modes, -1),
        lax.all_gather(right_y, "py", axis=0, tiled=True),
        preferred_element_type=jnp.float32,
    ).astype(jnp.bfloat16)
    back_pencil = jnp.transpose(back_flat.reshape(layers, modes, count_y, height), (2, 0, 3, 1))
    back_y = lax.all_to_all(back_pencil, "py", 0, 0, tiled=True)
    back_y = jnp.moveaxis(back_y, 0, 2).reshape(layers, height, -1)
    correction = jnp.einsum(
        "zyi,ix->zyx",
        lax.all_gather(back_y, "px", axis=2, tiled=True),
        right_x,
        preferred_element_type=jnp.float32,
    )

    mobility = jnp.zeros(regime_code.shape, jnp.float32)
    for regime in range(mobility_table.shape[0]):
        mobility = jnp.where(regime_code == regime, mobility_table[regime], mobility)
    flag_x = upwind_flag[0]
    flag_y = upwind_flag[1]

    def net(axis, dim, flag, at, count):
        forward = [(i, i + 1) for i in range(count - 1)]
        backward = [(i + 1, i) for i in range(count - 1)]
        first = lambda a: lax.slice_in_dim(a, 0, 1, axis=dim)
        last = lambda a: lax.slice_in_dim(a, a.shape[dim] - 1, None, axis=dim)
        rest = lambda a: lax.slice_in_dim(a, 1, None, axis=dim)
        head = lambda a: lax.slice_in_dim(a, 0, a.shape[dim] - 1, axis=dim)
        mobil_high = lax.ppermute(first(mobility), axis, backward)
        mobil_low, flag_low = lax.ppermute(
            (last(mobility), last(flag).astype(jnp.float32)), axis, forward
        )
        press_high = lax.ppermute(first(correction), axis, backward)
        press_low = lax.ppermute(last(correction), axis, forward)
        press_next = jnp.concatenate([rest(correction), press_high], axis=dim)
        mobil_next = jnp.concatenate([rest(mobility), mobil_high], axis=dim)
        flux_high = jnp.where(flag == 1, mobility, mobil_next) * (correction - press_next)
        place = lax.broadcasted_iota(jnp.int32, correction.shape, dim)
        edge = (at == count - 1) & (place == correction.shape[dim] - 1)
        flux_high = jnp.where(edge, 0.0, flux_high)
        flux_edge = jnp.where(flag_low > 0.5, mobil_low, first(mobility)) * (press_low - first(correction))
        flux_edge = jnp.where(at == 0, 0.0, flux_edge)
        flux_low = jnp.concatenate([flux_edge, head(flux_high)], axis=dim)
        return flux_high - flux_low

    balance = net("px", 2, flag_x, at_x, count_x) + net("py", 1, flag_y, at_y, count_y)
    return (correction, balance)


def solution(mesh):
    return jax.shard_map(
        shards,
        mesh=mesh,
        in_specs=(
            P(None, "py", "px"),
            P("px"),
            P("py"),
            P(),
            P(),
            P(None, "px"),
            P("py", None),
            P("py", None),
            P(None, "px"),
            P(None, "py", "px"),
            P(None, None, "py", "px"),
            P(),
        ),
        out_specs=(P(None, "py", "px"), P(None, "py", "px")),
        check_vma=False,
    )
```

```python
import jax
import jax.numpy as jnp
from jax import lax
from jax.experimental import pallas as pl
from jax.experimental.pallas import tpu as pltpu
from jax.sharding import PartitionSpec as P


def exchange(block, axis):
    count = lax.axis_size(axis)
    parts = [block]
    for k in range(1, count):
        parts.append(lax.ppermute(block, axis, [(s, s ^ k) for s in range(count)]))
    return parts


def in_exchange_order(matrix, axis):
    count = lax.axis_size(axis)
    own = lax.axis_index(axis)
    blocks = matrix.reshape(count, matrix.shape[0] // count, matrix.shape[1])
    return jnp.concatenate(
        [lax.dynamic_index_in_dim(blocks, own ^ k, 0, keepdims=False) for k in range(count)]
    )


def chip_gather(block, count, at):
    groups = [list(range(core, count, 2)) for core in range(2)]
    mine = lax.all_gather(block, "py", axis=0, axis_index_groups=groups)
    other = lax.ppermute(mine, "py", [(s, s ^ 1) for s in range(count)])
    even = jnp.stack([mine, other], axis=1)
    odd = jnp.stack([other, mine], axis=1)
    whole = jnp.where(at % 2 == 0, even, odd)
    return whole.reshape((-1,) + block.shape[1:])


def thomas_kernel(coupling_ref, shift_ref, ly_ref, lx_ref, rhs_ref, out_ref):
    layers = rhs_ref.shape[0]
    mode_sum = ly_ref[...] + lx_ref[...]
    ratios = []
    partial_values = []
    for layer_index in range(layers):
        diagonal = mode_sum + shift_ref[layer_index]
        if layer_index > 0:
            diagonal = diagonal + coupling_ref[layer_index - 1]
        if layer_index < layers - 1:
            diagonal = diagonal + coupling_ref[layer_index]
        if layer_index == 0:
            pivots = diagonal
            solved = rhs_ref[0] / pivots
        else:
            pivots = diagonal + coupling_ref[layer_index - 1] * ratios[-1]
            solved = (rhs_ref[layer_index] + coupling_ref[layer_index - 1] * partial_values[-1]) / pivots
        partial_values.append(solved)
        if layer_index < layers - 1:
            ratios.append(-coupling_ref[layer_index] / pivots)
    result = partial_values[layers - 1]
    out_ref[layers - 1] = result.astype(out_ref.dtype)
    for layer_index in range(layers - 2, -1, -1):
        result = partial_values[layer_index] - ratios[layer_index] * result
        out_ref[layer_index] = result.astype(out_ref.dtype)


def thomas_solve(rhs, lambda_x, lambda_y, coupling, layer_shift):
    layers, modes, rows = rhs.shape
    tile = min(rows, 512)
    smem = pl.BlockSpec(memory_space=pltpu.SMEM)
    return pl.pallas_call(
        thomas_kernel,
        grid=(rows // tile,),
        in_specs=[
            smem,
            smem,
            pl.BlockSpec((1, tile), lambda j: (0, j)),
            pl.BlockSpec((modes, 1), lambda j: (0, 0)),
            pl.BlockSpec((layers, modes, tile), lambda j: (0, 0, j)),
        ],
        out_specs=pl.BlockSpec((layers, modes, tile), lambda j: (0, 0, j)),
        out_shape=jax.ShapeDtypeStruct(rhs.shape, jnp.bfloat16),
    )(coupling, layer_shift, lambda_y.reshape(1, rows), lambda_x.reshape(modes, 1), rhs)


def shards(
    residual,
    lambda_x,
    lambda_y,
    coupling,
    layer_shift,
    left_x,
    left_y,
    right_y,
    right_x,
    regime_code,
    upwind_flag,
    mobility_table,
):
    count_x = lax.axis_size("px")
    count_y = lax.axis_size("py")
    at_x = lax.axis_index("px")
    at_y = lax.axis_index("py")
    layers, height, width = residual.shape
    modes = left_x.shape[1] // count_y

    rounded = residual.astype(jnp.bfloat16)
    spectral_x = jnp.einsum(
        "zyx,xci->czyi",
        jnp.concatenate(exchange(rounded, "px"), axis=2),
        in_exchange_order(left_x, "px").reshape(-1, count_y, modes),
        preferred_element_type=jnp.float32,
    ).astype(jnp.bfloat16)
    pencil = lax.all_to_all(spectral_x, "py", 0, 0, tiled=True)
    high = lax.reduce_precision(lambda_y, exponent_bits=8, mantissa_bits=7)
    rest = lambda_y - high
    middle = lax.reduce_precision(rest, exponent_bits=8, mantissa_bits=7)
    low = lax.reduce_precision(rest - middle, exponent_bits=8, mantissa_bits=7)
    high, middle, low = (p.astype(jnp.bfloat16) for p in (high, middle, low))
    pieces = jnp.zeros((lambda_y.shape[0], 128), jnp.bfloat16)
    pieces = pieces.at[:, 0].set(high).at[:, 1].set(middle).at[:, 2].set(low)
    carried = chip_gather(jnp.concatenate([left_y, pieces], axis=1), count_y, at_y)
    columns = left_y.shape[1]
    flat = jnp.transpose(pencil, (1, 3, 0, 2)).reshape(layers * modes, -1)
    spectral = jnp.einsum(
        "ny,jy->nj",
        flat,
        carried[:, :columns],
        preferred_element_type=jnp.float32,
    ).reshape(layers, modes, -1)
    own_x = lax.dynamic_slice_in_dim(lambda_x, at_y * modes, modes)
    got = carried[:, columns:columns + 3].astype(jnp.float32)
    all_y = got[:, 0] + (got[:, 1] + got[:, 2])
    solved = thomas_solve(spectral, own_x, all_y, coupling, layer_shift)
    back_flat = jnp.einsum(
        "nj,yj->ny",
        solved.reshape(layers * modes, -1),
        chip_gather(right_y, count_y, at_y),
        preferred_element_type=jnp.float32,
    ).astype(jnp.bfloat16)
    back_pencil = jnp.transpose(back_flat.reshape(layers, modes, count_y, height), (2, 0, 3, 1))
    back_y = lax.all_to_all(back_pencil, "py", 0, 0, tiled=True)
    back_y = jnp.moveaxis(back_y, 0, 2).reshape(layers, height, -1)
    correction = jnp.einsum(
        "zyi,ix->zyx",
        lax.all_gather(back_y, "px", axis=2, tiled=True),
        right_x,
        preferred_element_type=jnp.float32,
    )

    mobility = jnp.zeros(regime_code.shape, jnp.float32)
    for regime in range(mobility_table.shape[0]):
        mobility = jnp.where(regime_code == regime, mobility_table[regime], mobility)
    flag_x = upwind_flag[0]
    flag_y = upwind_flag[1]

    def net(axis, dim, flag, at, count):
        forward = [(i, i + 1) for i in range(count - 1)]
        backward = [(i + 1, i) for i in range(count - 1)]
        first = lambda a: lax.slice_in_dim(a, 0, 1, axis=dim)
        last = lambda a: lax.slice_in_dim(a, a.shape[dim] - 1, None, axis=dim)
        rest = lambda a: lax.slice_in_dim(a, 1, None, axis=dim)
        head = lambda a: lax.slice_in_dim(a, 0, a.shape[dim] - 1, axis=dim)
        high = lax.ppermute(jnp.stack([first(correction), first(mobility)]), axis, backward)
        low = lax.ppermute(
            jnp.stack([last(correction), last(mobility), last(flag).astype(jnp.float32)]), axis, forward
        )
        press_next = jnp.concatenate([rest(correction), high[0]], axis=dim)
        mobil_next = jnp.concatenate([rest(mobility), high[1]], axis=dim)
        flux_high = jnp.where(flag == 1, mobility, mobil_next) * (correction - press_next)
        place = lax.broadcasted_iota(jnp.int32, correction.shape, dim)
        edge = (at == count - 1) & (place == correction.shape[dim] - 1)
        flux_high = jnp.where(edge, 0.0, flux_high)
        flux_edge = jnp.where(low[2] > 0.5, low[1], first(mobility)) * (low[0] - first(correction))
        flux_edge = jnp.where(at == 0, 0.0, flux_edge)
        flux_low = jnp.concatenate([flux_edge, head(flux_high)], axis=dim)
        return flux_high - flux_low

    balance = net("px", 2, flag_x, at_x, count_x) + net("py", 1, flag_y, at_y, count_y)
    return (correction, balance)


def solution(mesh):
    return jax.shard_map(
        shards,
        mesh=mesh,
        in_specs=(
            P(None, "py", "px"),
            P("px"),
            P("py"),
            P(),
            P(),
            P(None, "px"),
            P("py", None),
            P("py", None),
            P(None, "px"),
            P(None, "py", "px"),
            P(None, None, "py", "px"),
            P(),
        ),
        out_specs=(P(None, "py", "px"), P(None, "py", "px")),
        check_vma=False,
    )
```

```python
import jax
import jax.numpy as jnp
from jax import lax
from jax.experimental import pallas as pl
from jax.experimental.pallas import tpu as pltpu
from jax.sharding import PartitionSpec as P


def exchange(block, axis):
    count = lax.axis_size(axis)
    parts = [block]
    for k in range(1, count):
        parts.append(lax.ppermute(block, axis, [(s, s ^ k) for s in range(count)]))
    return parts


def in_exchange_order(matrix, axis):
    count = lax.axis_size(axis)
    own = lax.axis_index(axis)
    blocks = matrix.reshape(count, matrix.shape[0] // count, matrix.shape[1])
    return jnp.concatenate(
        [lax.dynamic_index_in_dim(blocks, own ^ k, 0, keepdims=False) for k in range(count)]
    )


def thomas_kernel(coupling_ref, shift_ref, ly_ref, lx_ref, rhs_ref, out_ref):
    layers = rhs_ref.shape[0]
    mode_sum = ly_ref[...] + lx_ref[...]
    ratios = []
    partial_values = []
    for layer_index in range(layers):
        diagonal = mode_sum + shift_ref[layer_index]
        if layer_index > 0:
            diagonal = diagonal + coupling_ref[layer_index - 1]
        if layer_index < layers - 1:
            diagonal = diagonal + coupling_ref[layer_index]
        if layer_index == 0:
            pivots = diagonal
            solved = rhs_ref[0] / pivots
        else:
            pivots = diagonal + coupling_ref[layer_index - 1] * ratios[-1]
            solved = (rhs_ref[layer_index] + coupling_ref[layer_index - 1] * partial_values[-1]) / pivots
        partial_values.append(solved)
        if layer_index < layers - 1:
            ratios.append(-coupling_ref[layer_index] / pivots)
    result = partial_values[layers - 1]
    out_ref[layers - 1] = result.astype(out_ref.dtype)
    for layer_index in range(layers - 2, -1, -1):
        result = partial_values[layer_index] - ratios[layer_index] * result
        out_ref[layer_index] = result.astype(out_ref.dtype)


def thomas_solve(rhs, lambda_x, lambda_y, coupling, layer_shift):
    layers, modes, rows = rhs.shape
    tile = min(rows, 512)
    smem = pl.BlockSpec(memory_space=pltpu.SMEM)
    return pl.pallas_call(
        thomas_kernel,
        grid=(rows // tile,),
        in_specs=[
            smem,
            smem,
            pl.BlockSpec((1, tile), lambda j: (0, j)),
            pl.BlockSpec((modes, 1), lambda j: (0, 0)),
            pl.BlockSpec((layers, modes, tile), lambda j: (0, 0, j)),
        ],
        out_specs=pl.BlockSpec((layers, modes, tile), lambda j: (0, 0, j)),
        out_shape=jax.ShapeDtypeStruct(rhs.shape, jnp.bfloat16),
    )(coupling, layer_shift, lambda_y.reshape(1, rows), lambda_x.reshape(modes, 1), rhs)


def shards(
    residual,
    lambda_x,
    lambda_y,
    coupling,
    layer_shift,
    left_x,
    left_y,
    right_y,
    right_x,
    regime_code,
    upwind_flag,
    mobility_table,
):
    count_x = lax.axis_size("px")
    count_y = lax.axis_size("py")
    at_x = lax.axis_index("px")
    at_y = lax.axis_index("py")
    layers, height, width = residual.shape
    modes = left_x.shape[1] // count_y

    rounded = residual.astype(jnp.bfloat16)
    spectral_x = jnp.einsum(
        "zyx,xci->czyi",
        jnp.concatenate(exchange(rounded, "px"), axis=2),
        in_exchange_order(left_x, "px").reshape(-1, count_y, modes),
        preferred_element_type=jnp.float32,
    ).astype(jnp.bfloat16)
    pencil = lax.all_to_all(spectral_x, "py", 0, 0, tiled=True)
    high = lax.reduce_precision(lambda_y, exponent_bits=8, mantissa_bits=7)
    rest = lambda_y - high
    middle = lax.reduce_precision(rest, exponent_bits=8, mantissa_bits=7)
    low = lax.reduce_precision(rest - middle, exponent_bits=8, mantissa_bits=7)
    high, middle, low = (p.astype(jnp.bfloat16) for p in (high, middle, low))
    pieces = jnp.zeros((lambda_y.shape[0], 128), jnp.bfloat16)
    pieces = pieces.at[:, 0].set(high).at[:, 1].set(middle).at[:, 2].set(low)
    carried = lax.all_gather(jnp.concatenate([left_y, pieces, right_y], axis=1), "py", axis=0, tiled=True)
    columns = left_y.shape[1]
    right_all = carried[:, columns + pieces.shape[1]:]
    flat = jnp.transpose(pencil, (1, 3, 0, 2)).reshape(layers * modes, -1)
    spectral = jnp.einsum(
        "ny,jy->nj",
        flat,
        carried[:, :columns],
        preferred_element_type=jnp.float32,
    ).reshape(layers, modes, -1)
    own_x = lax.dynamic_slice_in_dim(lambda_x, at_y * modes, modes)
    got = carried[:, columns:columns + 3].astype(jnp.float32)
    all_y = got[:, 0] + (got[:, 1] + got[:, 2])
    solved = thomas_solve(spectral, own_x, all_y, coupling, layer_shift)
    back_flat = jnp.einsum(
        "nj,yj->ny",
        solved.reshape(layers * modes, -1),
        right_all,
        preferred_element_type=jnp.float32,
    ).astype(jnp.bfloat16)
    back_pencil = jnp.transpose(back_flat.reshape(layers, modes, count_y, height), (2, 0, 3, 1))
    back_y = lax.all_to_all(back_pencil, "py", 0, 0, tiled=True)
    back_y = jnp.moveaxis(back_y, 0, 2).reshape(layers, height, -1)
    correction = jnp.einsum(
        "zyi,ix->zyx",
        lax.all_gather(back_y, "px", axis=2, tiled=True),
        right_x,
        preferred_element_type=jnp.float32,
    )

    mobility = jnp.zeros(regime_code.shape, jnp.float32)
    for regime in range(mobility_table.shape[0]):
        mobility = jnp.where(regime_code == regime, mobility_table[regime], mobility)
    flag_x = upwind_flag[0]
    flag_y = upwind_flag[1]

    def net(axis, dim, flag, at, count):
        forward = [(i, i + 1) for i in range(count - 1)]
        backward = [(i + 1, i) for i in range(count - 1)]
        first = lambda a: lax.slice_in_dim(a, 0, 1, axis=dim)
        last = lambda a: lax.slice_in_dim(a, a.shape[dim] - 1, None, axis=dim)
        rest = lambda a: lax.slice_in_dim(a, 1, None, axis=dim)
        head = lambda a: lax.slice_in_dim(a, 0, a.shape[dim] - 1, axis=dim)
        high = lax.ppermute(jnp.stack([first(correction), first(mobility)]), axis, backward)
        low = lax.ppermute(
            jnp.stack([last(correction), last(mobility), last(flag).astype(jnp.float32)]), axis, forward
        )
        press_next = jnp.concatenate([rest(correction), high[0]], axis=dim)
        mobil_next = jnp.concatenate([rest(mobility), high[1]], axis=dim)
        flux_high = jnp.where(flag == 1, mobility, mobil_next) * (correction - press_next)
        place = lax.broadcasted_iota(jnp.int32, correction.shape, dim)
        edge = (at == count - 1) & (place == correction.shape[dim] - 1)
        flux_high = jnp.where(edge, 0.0, flux_high)
        flux_edge = jnp.where(low[2] > 0.5, low[1], first(mobility)) * (low[0] - first(correction))
        flux_edge = jnp.where(at == 0, 0.0, flux_edge)
        flux_low = jnp.concatenate([flux_edge, head(flux_high)], axis=dim)
        return flux_high - flux_low

    balance = net("px", 2, flag_x, at_x, count_x) + net("py", 1, flag_y, at_y, count_y)
    return (correction, balance)


def solution(mesh):
    return jax.shard_map(
        shards,
        mesh=mesh,
        in_specs=(
            P(None, "py", "px"),
            P("px"),
            P("py"),
            P(),
            P(),
            P(None, "px"),
            P("py", None),
            P("py", None),
            P(None, "px"),
            P(None, "py", "px"),
            P(None, None, "py", "px"),
            P(),
        ),
        out_specs=(P(None, "py", "px"), P(None, "py", "px")),
        check_vma=False,
    )
```

```python
import jax
import jax.numpy as jnp
from jax import lax
from jax.experimental import pallas as pl
from jax.experimental.pallas import tpu as pltpu
from jax.sharding import PartitionSpec as P


def exchange(block, axis):
    count = lax.axis_size(axis)
    parts = [block]
    for k in range(1, count):
        parts.append(lax.ppermute(block, axis, [(s, s ^ k) for s in range(count)]))
    return parts


def in_exchange_order(matrix, axis):
    count = lax.axis_size(axis)
    own = lax.axis_index(axis)
    blocks = matrix.reshape(count, matrix.shape[0] // count, matrix.shape[1])
    return jnp.concatenate(
        [lax.dynamic_index_in_dim(blocks, own ^ k, 0, keepdims=False) for k in range(count)]
    )


def thomas_kernel(coupling_ref, shift_ref, ly_ref, lx_ref, rhs_ref, out_ref):
    layers = rhs_ref.shape[0]
    mode_sum = ly_ref[...] + lx_ref[...]
    ratios = []
    partial_values = []
    for layer_index in range(layers):
        diagonal = mode_sum + shift_ref[layer_index]
        if layer_index > 0:
            diagonal = diagonal + coupling_ref[layer_index - 1]
        if layer_index < layers - 1:
            diagonal = diagonal + coupling_ref[layer_index]
        if layer_index == 0:
            pivots = diagonal
            solved = rhs_ref[0] / pivots
        else:
            pivots = diagonal + coupling_ref[layer_index - 1] * ratios[-1]
            solved = (rhs_ref[layer_index] + coupling_ref[layer_index - 1] * partial_values[-1]) / pivots
        partial_values.append(solved)
        if layer_index < layers - 1:
            ratios.append(-coupling_ref[layer_index] / pivots)
    result = partial_values[layers - 1]
    out_ref[layers - 1] = result.astype(out_ref.dtype)
    for layer_index in range(layers - 2, -1, -1):
        result = partial_values[layer_index] - ratios[layer_index] * result
        out_ref[layer_index] = result.astype(out_ref.dtype)


def thomas_solve(rhs, lambda_x, lambda_y, coupling, layer_shift):
    layers, modes, rows = rhs.shape
    tile = min(rows, 512)
    smem = pl.BlockSpec(memory_space=pltpu.SMEM)
    return pl.pallas_call(
        thomas_kernel,
        grid=(rows // tile,),
        in_specs=[
            smem,
            smem,
            pl.BlockSpec((1, tile), lambda j: (0, j)),
            pl.BlockSpec((modes, 1), lambda j: (0, 0)),
            pl.BlockSpec((layers, modes, tile), lambda j: (0, 0, j)),
        ],
        out_specs=pl.BlockSpec((layers, modes, tile), lambda j: (0, 0, j)),
        out_shape=jax.ShapeDtypeStruct(rhs.shape, jnp.bfloat16),
    )(coupling, layer_shift, lambda_y.reshape(1, rows), lambda_x.reshape(modes, 1), rhs)


def shards(
    residual,
    lambda_x,
    lambda_y,
    coupling,
    layer_shift,
    left_x,
    left_y,
    right_y,
    right_x,
    regime_code,
    upwind_flag,
    mobility_table,
):
    count_x = lax.axis_size("px")
    count_y = lax.axis_size("py")
    at_x = lax.axis_index("px")
    at_y = lax.axis_index("py")
    layers, height, width = residual.shape
    modes = left_x.shape[1] // count_y

    rounded = residual.astype(jnp.bfloat16)
    weights_x = in_exchange_order(left_x, "px").reshape(count_x, width, count_y, modes)
    blocks = exchange(rounded, "px")
    spectral_x = jnp.einsum("zyx,xci->czyi", blocks[0], weights_x[0], preferred_element_type=jnp.float32)
    for k in range(1, count_x):
        spectral_x = spectral_x + jnp.einsum(
            "zyx,xci->czyi", blocks[k], weights_x[k], preferred_element_type=jnp.float32
        )
    spectral_x = spectral_x.astype(jnp.bfloat16)
    pencil = lax.all_to_all(spectral_x, "py", 0, 0, tiled=True)
    high = lax.reduce_precision(lambda_y, exponent_bits=8, mantissa_bits=7)
    rest = lambda_y - high
    middle = lax.reduce_precision(rest, exponent_bits=8, mantissa_bits=7)
    low = lax.reduce_precision(rest - middle, exponent_bits=8, mantissa_bits=7)
    high, middle, low = (p.astype(jnp.bfloat16) for p in (high, middle, low))
    pieces = jnp.zeros((lambda_y.shape[0], 128), jnp.bfloat16)
    pieces = pieces.at[:, 0].set(high).at[:, 1].set(middle).at[:, 2].set(low)
    carried = lax.all_gather(jnp.concatenate([left_y, pieces, right_y], axis=1), "py", axis=0, tiled=True)
    columns = left_y.shape[1]
    right_all = carried[:, columns + pieces.shape[1]:]
    flat = jnp.transpose(pencil, (1, 3, 0, 2)).reshape(layers * modes, -1)
    spectral = jnp.einsum(
        "ny,jy->nj",
        flat,
        carried[:, :columns],
        preferred_element_type=jnp.float32,
    ).reshape(layers, modes, -1)
    own_x = lax.dynamic_slice_in_dim(lambda_x, at_y * modes, modes)
    got = carried[:, columns:columns + 3].astype(jnp.float32)
    all_y = got[:, 0] + (got[:, 1] + got[:, 2])
    solved = thomas_solve(spectral, own_x, all_y, coupling, layer_shift)
    back_flat = jnp.einsum(
        "nj,yj->ny",
        solved.reshape(layers * modes, -1),
        right_all,
        preferred_element_type=jnp.float32,
    ).astype(jnp.bfloat16)
    back_pencil = jnp.transpose(back_flat.reshape(layers, modes, count_y, height), (2, 0, 3, 1))
    back_y = lax.all_to_all(back_pencil, "py", 0, 0, tiled=True)
    back_y = jnp.moveaxis(back_y, 0, 2).reshape(layers, height, -1)
    correction = jnp.einsum(
        "zyi,ix->zyx",
        lax.all_gather(back_y, "px", axis=2, tiled=True),
        right_x,
        preferred_element_type=jnp.float32,
    )

    mobility = jnp.zeros(regime_code.shape, jnp.float32)
    for regime in range(mobility_table.shape[0]):
        mobility = jnp.where(regime_code == regime, mobility_table[regime], mobility)
    flag_x = upwind_flag[0]
    flag_y = upwind_flag[1]

    def net(axis, dim, flag, at, count):
        forward = [(i, i + 1) for i in range(count - 1)]
        backward = [(i + 1, i) for i in range(count - 1)]
        first = lambda a: lax.slice_in_dim(a, 0, 1, axis=dim)
        last = lambda a: lax.slice_in_dim(a, a.shape[dim] - 1, None, axis=dim)
        rest = lambda a: lax.slice_in_dim(a, 1, None, axis=dim)
        head = lambda a: lax.slice_in_dim(a, 0, a.shape[dim] - 1, axis=dim)
        high = lax.ppermute(jnp.stack([first(correction), first(mobility)]), axis, backward)
        low = lax.ppermute(
            jnp.stack([last(correction), last(mobility), last(flag).astype(jnp.float32)]), axis, forward
        )
        press_next = jnp.concatenate([rest(correction), high[0]], axis=dim)
        mobil_next = jnp.concatenate([rest(mobility), high[1]], axis=dim)
        flux_high = jnp.where(flag == 1, mobility, mobil_next) * (correction - press_next)
        place = lax.broadcasted_iota(jnp.int32, correction.shape, dim)
        edge = (at == count - 1) & (place == correction.shape[dim] - 1)
        flux_high = jnp.where(edge, 0.0, flux_high)
        flux_edge = jnp.where(low[2] > 0.5, low[1], first(mobility)) * (low[0] - first(correction))
        flux_edge = jnp.where(at == 0, 0.0, flux_edge)
        flux_low = jnp.concatenate([flux_edge, head(flux_high)], axis=dim)
        return flux_high - flux_low

    balance = net("px", 2, flag_x, at_x, count_x) + net("py", 1, flag_y, at_y, count_y)
    return (correction, balance)


def solution(mesh):
    return jax.shard_map(
        shards,
        mesh=mesh,
        in_specs=(
            P(None, "py", "px"),
            P("px"),
            P("py"),
            P(),
            P(),
            P(None, "px"),
            P("py", None),
            P("py", None),
            P(None, "px"),
            P(None, "py", "px"),
            P(None, None, "py", "px"),
            P(),
        ),
        out_specs=(P(None, "py", "px"), P(None, "py", "px")),
        check_vma=False,
    )
```

```python
import jax
import jax.numpy as jnp
from jax import lax
from jax.experimental import pallas as pl
from jax.experimental.pallas import tpu as pltpu
from jax.sharding import PartitionSpec as P


def exchange(block, axis):
    count = lax.axis_size(axis)
    parts = [block]
    for k in range(1, count):
        parts.append(lax.ppermute(block, axis, [(s, s ^ k) for s in range(count)]))
    return parts


def in_exchange_order(matrix, axis):
    count = lax.axis_size(axis)
    own = lax.axis_index(axis)
    blocks = matrix.reshape(count, matrix.shape[0] // count, matrix.shape[1])
    return jnp.concatenate(
        [lax.dynamic_index_in_dim(blocks, own ^ k, 0, keepdims=False) for k in range(count)]
    )


def thomas_kernel(coupling_ref, shift_ref, ly_ref, lx_ref, rhs_ref, out_ref):
    layers = rhs_ref.shape[0]
    mode_sum = ly_ref[...] + lx_ref[...]
    ratios = []
    partial_values = []
    for layer_index in range(layers):
        diagonal = mode_sum + shift_ref[layer_index]
        if layer_index > 0:
            diagonal = diagonal + coupling_ref[layer_index - 1]
        if layer_index < layers - 1:
            diagonal = diagonal + coupling_ref[layer_index]
        if layer_index == 0:
            pivots = diagonal
            solved = rhs_ref[0] / pivots
        else:
            pivots = diagonal + coupling_ref[layer_index - 1] * ratios[-1]
            solved = (rhs_ref[layer_index] + coupling_ref[layer_index - 1] * partial_values[-1]) / pivots
        partial_values.append(solved)
        if layer_index < layers - 1:
            ratios.append(-coupling_ref[layer_index] / pivots)
    result = partial_values[layers - 1]
    out_ref[layers - 1] = result.astype(out_ref.dtype)
    for layer_index in range(layers - 2, -1, -1):
        result = partial_values[layer_index] - ratios[layer_index] * result
        out_ref[layer_index] = result.astype(out_ref.dtype)


def thomas_solve(rhs, lambda_x, lambda_y, coupling, layer_shift):
    layers, modes, rows = rhs.shape
    tile = min(rows, 512)
    smem = pl.BlockSpec(memory_space=pltpu.SMEM)
    return pl.pallas_call(
        thomas_kernel,
        grid=(rows // tile,),
        in_specs=[
            smem,
            smem,
            pl.BlockSpec((1, tile), lambda j: (0, j)),
            pl.BlockSpec((modes, 1), lambda j: (0, 0)),
            pl.BlockSpec((layers, modes, tile), lambda j: (0, 0, j)),
        ],
        out_specs=pl.BlockSpec((layers, modes, tile), lambda j: (0, 0, j)),
        out_shape=jax.ShapeDtypeStruct(rhs.shape, jnp.bfloat16),
    )(coupling, layer_shift, lambda_y.reshape(1, rows), lambda_x.reshape(modes, 1), rhs)


def shards(
    residual,
    lambda_x,
    lambda_y,
    coupling,
    layer_shift,
    left_x,
    left_y,
    right_y,
    right_x,
    regime_code,
    upwind_flag,
    mobility_table,
):
    count_x = lax.axis_size("px")
    count_y = lax.axis_size("py")
    at_x = lax.axis_index("px")
    at_y = lax.axis_index("py")
    layers, height, width = residual.shape
    modes = left_x.shape[1] // count_y

    rounded = residual.astype(jnp.bfloat16)
    spectral_x = jnp.einsum(
        "zyx,xci->czyi",
        jnp.concatenate(exchange(rounded, "px"), axis=2),
        in_exchange_order(left_x, "px").reshape(-1, count_y, modes),
        preferred_element_type=jnp.float32,
    ).astype(jnp.bfloat16)
    pencil = lax.all_to_all(spectral_x, "py", 0, 0, tiled=True)
    high = lax.reduce_precision(lambda_y, exponent_bits=8, mantissa_bits=7)
    rest = lambda_y - high
    middle = lax.reduce_precision(rest, exponent_bits=8, mantissa_bits=7)
    low = lax.reduce_precision(rest - middle, exponent_bits=8, mantissa_bits=7)
    high, middle, low = (p.astype(jnp.bfloat16) for p in (high, middle, low))
    pieces = jnp.zeros((lambda_y.shape[0], 128), jnp.bfloat16)
    pieces = pieces.at[:, 0].set(high).at[:, 1].set(middle).at[:, 2].set(low)
    carried = lax.all_gather(jnp.concatenate([left_y, pieces, right_y], axis=1), "py", axis=0, tiled=True)
    columns = left_y.shape[1]
    right_all = carried[:, columns + pieces.shape[1]:]
    flat = jnp.transpose(pencil, (1, 3, 0, 2)).reshape(layers * modes, -1)
    spectral = jnp.einsum(
        "ny,jy->nj",
        flat,
        carried[:, :columns],
        preferred_element_type=jnp.float32,
    ).reshape(layers, modes, -1)
    own_x = lax.dynamic_slice_in_dim(lambda_x, at_y * modes, modes)
    got = carried[:, columns:columns + 3].astype(jnp.float32)
    all_y = got[:, 0] + (got[:, 1] + got[:, 2])
    solved = thomas_solve(spectral, own_x, all_y, coupling, layer_shift)
    back_flat = jnp.einsum(
        "nj,yj->ny",
        solved.reshape(layers * modes, -1),
        right_all,
        preferred_element_type=jnp.float32,
    ).astype(jnp.bfloat16)
    back_pencil = jnp.transpose(back_flat.reshape(layers, modes, count_y, height), (2, 0, 3, 1))
    split = layers // 2
    gathered = []
    for lo, hi in ((0, split), (split, layers)):
        part = lax.all_to_all(back_pencil[:, lo:hi], "py", 0, 0, tiled=True)
        part = jnp.moveaxis(part, 0, 2).reshape(hi - lo, height, -1)
        gathered.append(lax.all_gather(part, "px", axis=2, tiled=True))
    correction = jnp.einsum(
        "zyi,ix->zyx",
        jnp.concatenate(gathered),
        right_x,
        preferred_element_type=jnp.float32,
    )

    mobility = jnp.zeros(regime_code.shape, jnp.float32)
    for regime in range(mobility_table.shape[0]):
        mobility = jnp.where(regime_code == regime, mobility_table[regime], mobility)
    flag_x = upwind_flag[0]
    flag_y = upwind_flag[1]

    def net(axis, dim, flag, at, count):
        forward = [(i, i + 1) for i in range(count - 1)]
        backward = [(i + 1, i) for i in range(count - 1)]
        first = lambda a: lax.slice_in_dim(a, 0, 1, axis=dim)
        last = lambda a: lax.slice_in_dim(a, a.shape[dim] - 1, None, axis=dim)
        rest = lambda a: lax.slice_in_dim(a, 1, None, axis=dim)
        head = lambda a: lax.slice_in_dim(a, 0, a.shape[dim] - 1, axis=dim)
        high = lax.ppermute(jnp.stack([first(correction), first(mobility)]), axis, backward)
        low = lax.ppermute(
            jnp.stack([last(correction), last(mobility), last(flag).astype(jnp.float32)]), axis, forward
        )
        press_next = jnp.concatenate([rest(correction), high[0]], axis=dim)
        mobil_next = jnp.concatenate([rest(mobility), high[1]], axis=dim)
        flux_high = jnp.where(flag == 1, mobility, mobil_next) * (correction - press_next)
        place = lax.broadcasted_iota(jnp.int32, correction.shape, dim)
        edge = (at == count - 1) & (place == correction.shape[dim] - 1)
        flux_high = jnp.where(edge, 0.0, flux_high)
        flux_edge = jnp.where(low[2] > 0.5, low[1], first(mobility)) * (low[0] - first(correction))
        flux_edge = jnp.where(at == 0, 0.0, flux_edge)
        flux_low = jnp.concatenate([flux_edge, head(flux_high)], axis=dim)
        return flux_high - flux_low

    balance = net("px", 2, flag_x, at_x, count_x) + net("py", 1, flag_y, at_y, count_y)
    return (correction, balance)


def solution(mesh):
    return jax.shard_map(
        shards,
        mesh=mesh,
        in_specs=(
            P(None, "py", "px"),
            P("px"),
            P("py"),
            P(),
            P(),
            P(None, "px"),
            P("py", None),
            P("py", None),
            P(None, "px"),
            P(None, "py", "px"),
            P(None, None, "py", "px"),
            P(),
        ),
        out_specs=(P(None, "py", "px"), P(None, "py", "px")),
        check_vma=False,
    )
```

```python
import jax
import jax.numpy as jnp
from jax import lax
from jax.experimental import pallas as pl
from jax.experimental.pallas import tpu as pltpu
from jax.sharding import PartitionSpec as P


def exchange(block, axis):
    count = lax.axis_size(axis)
    parts = [block]
    for k in range(1, count):
        parts.append(lax.ppermute(block, axis, [(s, s ^ k) for s in range(count)]))
    return parts


def in_exchange_order(matrix, axis):
    count = lax.axis_size(axis)
    own = lax.axis_index(axis)
    blocks = matrix.reshape(count, matrix.shape[0] // count, matrix.shape[1])
    return jnp.concatenate(
        [lax.dynamic_index_in_dim(blocks, own ^ k, 0, keepdims=False) for k in range(count)]
    )


def thomas_kernel(coupling_ref, shift_ref, ly_ref, lx_ref, rhs_ref, out_ref):
    layers = rhs_ref.shape[0]
    mode_sum = ly_ref[...] + lx_ref[...]
    ratios = []
    partial_values = []
    for layer_index in range(layers):
        diagonal = mode_sum + shift_ref[layer_index]
        if layer_index > 0:
            diagonal = diagonal + coupling_ref[layer_index - 1]
        if layer_index < layers - 1:
            diagonal = diagonal + coupling_ref[layer_index]
        if layer_index == 0:
            pivots = diagonal
            solved = rhs_ref[0] / pivots
        else:
            pivots = diagonal + coupling_ref[layer_index - 1] * ratios[-1]
            solved = (rhs_ref[layer_index] + coupling_ref[layer_index - 1] * partial_values[-1]) / pivots
        partial_values.append(solved)
        if layer_index < layers - 1:
            ratios.append(-coupling_ref[layer_index] / pivots)
    result = partial_values[layers - 1]
    out_ref[layers - 1] = result.astype(out_ref.dtype)
    for layer_index in range(layers - 2, -1, -1):
        result = partial_values[layer_index] - ratios[layer_index] * result
        out_ref[layer_index] = result.astype(out_ref.dtype)


def thomas_solve(rhs, lambda_x, lambda_y, coupling, layer_shift):
    layers, modes, rows = rhs.shape
    tile = min(rows, 512)
    smem = pl.BlockSpec(memory_space=pltpu.SMEM)
    return pl.pallas_call(
        thomas_kernel,
        grid=(rows // tile,),
        in_specs=[
            smem,
            smem,
            pl.BlockSpec((1, tile), lambda j: (0, j)),
            pl.BlockSpec((modes, 1), lambda j: (0, 0)),
            pl.BlockSpec((layers, modes, tile), lambda j: (0, 0, j)),
        ],
        out_specs=pl.BlockSpec((layers, modes, tile), lambda j: (0, 0, j)),
        out_shape=jax.ShapeDtypeStruct(rhs.shape, jnp.bfloat16),
    )(coupling, layer_shift, lambda_y.reshape(1, rows), lambda_x.reshape(modes, 1), rhs)


def shards(
    residual,
    lambda_x,
    lambda_y,
    coupling,
    layer_shift,
    left_x,
    left_y,
    right_y,
    right_x,
    regime_code,
    upwind_flag,
    mobility_table,
):
    count_x = lax.axis_size("px")
    count_y = lax.axis_size("py")
    at_x = lax.axis_index("px")
    at_y = lax.axis_index("py")
    layers, height, width = residual.shape
    modes = left_x.shape[1] // count_y

    rounded = residual.astype(jnp.bfloat16)
    spectral_x = jnp.einsum(
        "zyx,xci->czyi",
        jnp.concatenate(exchange(rounded, "px"), axis=2),
        in_exchange_order(left_x, "px").reshape(-1, count_y, modes),
        preferred_element_type=jnp.float32,
    ).astype(jnp.bfloat16)
    pencil = lax.all_to_all(spectral_x, "py", 0, 0, tiled=True)
    high = lax.reduce_precision(lambda_y, exponent_bits=8, mantissa_bits=7)
    rest = lambda_y - high
    middle = lax.reduce_precision(rest, exponent_bits=8, mantissa_bits=7)
    low = lax.reduce_precision(rest - middle, exponent_bits=8, mantissa_bits=7)
    high, middle, low = (p.astype(jnp.bfloat16) for p in (high, middle, low))
    pieces = jnp.zeros((lambda_y.shape[0], 128), jnp.bfloat16)
    pieces = pieces.at[:, 0].set(high).at[:, 1].set(middle).at[:, 2].set(low)
    carried = lax.all_gather(jnp.concatenate([left_y, pieces, right_y], axis=1), "py", axis=0, tiled=True)
    columns = left_y.shape[1]
    right_all = carried[:, columns + pieces.shape[1]:]
    flat = jnp.transpose(pencil, (1, 3, 0, 2)).reshape(layers * modes, -1)
    spectral = jnp.einsum(
        "ny,jy->nj",
        flat,
        carried[:, :columns],
        preferred_element_type=jnp.float32,
    ).reshape(layers, modes, -1)
    own_x = lax.dynamic_slice_in_dim(lambda_x, at_y * modes, modes)
    got = carried[:, columns:columns + 3].astype(jnp.float32)
    all_y = got[:, 0] + (got[:, 1] + got[:, 2])
    solved = thomas_solve(spectral, own_x, all_y, coupling, layer_shift)
    back_flat = jnp.einsum(
        "nj,yj->ny",
        solved.reshape(layers * modes, -1),
        right_all,
        preferred_element_type=jnp.float32,
    ).astype(jnp.bfloat16)
    back_pencil = jnp.transpose(back_flat.reshape(layers, modes, count_y, height), (2, 0, 3, 1))
    split = layers // 2
    gathered = []
    for lo, hi in ((0, layers // 3), (layers // 3, 2 * layers // 3), (2 * layers // 3, layers)):
        part = lax.all_to_all(back_pencil[:, lo:hi], "py", 0, 0, tiled=True)
        part = jnp.moveaxis(part, 0, 2).reshape(hi - lo, height, -1)
        gathered.append(lax.all_gather(part, "px", axis=2, tiled=True))
    correction = jnp.einsum(
        "zyi,ix->zyx",
        jnp.concatenate(gathered),
        right_x,
        preferred_element_type=jnp.float32,
    )

    mobility = jnp.zeros(regime_code.shape, jnp.float32)
    for regime in range(mobility_table.shape[0]):
        mobility = jnp.where(regime_code == regime, mobility_table[regime], mobility)
    flag_x = upwind_flag[0]
    flag_y = upwind_flag[1]

    def net(axis, dim, flag, at, count):
        forward = [(i, i + 1) for i in range(count - 1)]
        backward = [(i + 1, i) for i in range(count - 1)]
        first = lambda a: lax.slice_in_dim(a, 0, 1, axis=dim)
        last = lambda a: lax.slice_in_dim(a, a.shape[dim] - 1, None, axis=dim)
        rest = lambda a: lax.slice_in_dim(a, 1, None, axis=dim)
        head = lambda a: lax.slice_in_dim(a, 0, a.shape[dim] - 1, axis=dim)
        high = lax.ppermute(jnp.stack([first(correction), first(mobility)]), axis, backward)
        low = lax.ppermute(
            jnp.stack([last(correction), last(mobility), last(flag).astype(jnp.float32)]), axis, forward
        )
        press_next = jnp.concatenate([rest(correction), high[0]], axis=dim)
        mobil_next = jnp.concatenate([rest(mobility), high[1]], axis=dim)
        flux_high = jnp.where(flag == 1, mobility, mobil_next) * (correction - press_next)
        place = lax.broadcasted_iota(jnp.int32, correction.shape, dim)
        edge = (at == count - 1) & (place == correction.shape[dim] - 1)
        flux_high = jnp.where(edge, 0.0, flux_high)
        flux_edge = jnp.where(low[2] > 0.5, low[1], first(mobility)) * (low[0] - first(correction))
        flux_edge = jnp.where(at == 0, 0.0, flux_edge)
        flux_low = jnp.concatenate([flux_edge, head(flux_high)], axis=dim)
        return flux_high - flux_low

    balance = net("px", 2, flag_x, at_x, count_x) + net("py", 1, flag_y, at_y, count_y)
    return (correction, balance)


def solution(mesh):
    return jax.shard_map(
        shards,
        mesh=mesh,
        in_specs=(
            P(None, "py", "px"),
            P("px"),
            P("py"),
            P(),
            P(),
            P(None, "px"),
            P("py", None),
            P("py", None),
            P(None, "px"),
            P(None, "py", "px"),
            P(None, None, "py", "px"),
            P(),
        ),
        out_specs=(P(None, "py", "px"), P(None, "py", "px")),
        check_vma=False,
    )
```
